768 devices in a mesh: gx: 96 (over z, x, core), gy: 8 (over y).
Axes of the slice: x: 4, y: 8, z: 12, core: 2. Of those that a mesh axis runs over, the one named last changes fastest.
Arguments:
- queries: bfloat16 [1536, 256, 128], P('gx', 'gy'), may hold values from -6 to 6
- keys: bfloat16 [1536, 256, 128], P('gx', 'gy'), may hold values from -6 to 6
- values: bfloat16 [1536, 256, 128], P('gx', 'gy'), may hold values from -6 to 6
- out_attn: bfloat16 [1536, 256, 128], P('gx', 'gy'), may hold values from -6 to 6
- out_grad: bfloat16 [1536, 256, 128], P('gx', 'gy'), may hold values from -6 to 6
- log_norm: bfloat16 [4, 1536, 256], P(None, 'gx', 'gy'), may hold values from 3 to 4
- neighbour_blocks: int32 [96, 32, 3], P('gx', 'gy'), may hold values from 0 to 31, as said below
- stencil: float32 [5, 128], replicated, may hold values from -3 to 3
Outputs:
- query_grad: bfloat16 [1536, 256, 128], P('gx', 'gy')
- key_grad: bfloat16 [1536, 256, 128], P('gx', 'gy')
- value_grad: bfloat16 [1536, 256, 128], P('gx', 'gy')
- stencil_grad: float32 [5, 128], replicated
The draws below stay inside these ranges and needn't reach their ends.
Inputs may be any that keep to these rules, and one draw needn't show every extreme that they name: `neighbour_blocks`: among the entries of the 4 row blocks of one tile, at most 2 name blocks of any one tile of the strip (the tile of block c is c // 4), and exactly 2 do for some tile.
All inputs are finite; a program needn't handle non-finite values.
Results may differ from the reference program's by a relative error of at most 0.0054.
Values may be sent and summed in bfloat16 or wider, within the bound.
No kernel may reach another device: no remote copies, remote signals or barrier semaphores. Data moves between devices by JAX's collectives and lax.ppermute only.
A program may use at most 32 MiB of HBM per device.

```python
import math
import jax
import jax.numpy as jnp
from jax import lax

PX = 16
PY = 32
BLOCK = 128
HEADS = 4
NB = 3
F = 128
RB = 4
GRID_X = 1536
GRID_Y = 256
N_GX = 96
N_GY = 8


def draw_neighbour_blocks(key, part):
    row_blocks = PX * PY // BLOCK
    pair_count = row_blocks * NB
    capacity = max(2, (pair_count + N_GY - 1) // N_GY)
    first, second, third, fourth, fifth = jax.random.split(jax.random.fold_in(key, 11), 5)
    hot_base = jax.random.randint(first, (N_GX, 1), 0, N_GY)
    coin = jax.random.randint(second, (N_GX, N_GY), 0, 2)
    other = jax.random.randint(third, (N_GX, N_GY), 0, N_GY)
    hottest = jnp.where(coin == 0, hot_base, other)
    perm_keys = jax.random.split(fourth, N_GX * N_GY)
    orders = jax.vmap(lambda single: jax.random.permutation(single, pair_count))(perm_keys)
    orders = orders.reshape(N_GX, N_GY, pair_count).astype(jnp.int32)
    group = orders // capacity
    owner = (hottest[..., None] + group) % N_GY
    inner = jax.random.randint(fifth, (N_GX, N_GY, pair_count), 0, row_blocks)
    columns = owner * row_blocks + inner
    return columns.reshape(N_GX, N_GY * row_blocks, NB).astype(jnp.int32)


def block_levels(key, dims, shards, least, top_value):
    gain = 1.0
    for position, shards_of in shards:
        steps = jax.random.uniform(jax.random.fold_in(jax.random.fold_in(key, 6), position), (shards_of,), jnp.float32, least / len(shards), top_value / len(shards))
        gain = gain * jnp.repeat(jnp.exp(steps), dims[position] // shards_of).reshape((-1,) + (1,) * (len(dims) - 1 - position))
    return gain


def bell_draw(own_key, extent, scale, reach, shards=(), kind=jnp.bfloat16):
    level = block_levels(own_key, extent, shards, -0.22, 0.18) if shards else 1.0
    entries = jax.random.normal(own_key, extent, jnp.float32) * scale * level
    return jnp.minimum(jnp.maximum(entries, -reach), reach).astype(kind)


def setup_inputs(seed: int = 0) -> dict:
    streams_of = jax.random.split(jax.random.key(seed), 9)
    return {
        "queries": bell_draw(streams_of[0], (GRID_X, GRID_Y, F), 1.0, 6.0, ((0, 96), (1, 8))),
        "keys": bell_draw(streams_of[1], (GRID_X, GRID_Y, F), 1.0, 6.0, ((0, 96), (1, 8))),
        "values": bell_draw(streams_of[2], (GRID_X, GRID_Y, F), 1.0, 6.0, ((0, 96), (1, 8))),
        "out_attn": bell_draw(streams_of[3], (GRID_X, GRID_Y, F), 1.0, 6.0, ((0, 96), (1, 8))),
        "out_grad": bell_draw(streams_of[4], (GRID_X, GRID_Y, F), 1.0, 6.0, ((0, 96), (1, 8))),
        "log_norm": jnp.clip(3.0 + 1.0 * jax.random.uniform(streams_of[5], (HEADS, GRID_X, GRID_Y), jnp.float32) ** block_levels(streams_of[5], (HEADS, GRID_X, GRID_Y), ((1, 96), (2, 8)), -0.2, 0.2), 3.0, 4.0).astype(jnp.bfloat16),
        "neighbour_blocks": draw_neighbour_blocks(jax.random.fold_in(streams_of[8], 71), 0),
        "stencil": bell_draw(streams_of[7], (5, F), 0.5, 3.0, (), jnp.float32),
    }


def tile_grads(query_rows, grad_rows, stat_rows, key_rows, value_rows, head_count):
    item_count = query_rows.shape[0]
    block_rows = query_rows.shape[1]
    features = query_rows.shape[2]
    head_width = features // head_count
    softmax_scale = 1.0 / math.sqrt(head_width)
    shape_four = (item_count, block_rows, head_count, head_width)
    query_heads = query_rows.reshape(shape_four).astype(jnp.float32)
    grad_heads = grad_rows.reshape(shape_four).astype(jnp.float32)
    key_heads = key_rows.reshape(shape_four).astype(jnp.float32)
    value_heads = value_rows.reshape(shape_four).astype(jnp.float32)
    log_part = stat_rows[:, 0].astype(jnp.float32)
    delta_part = stat_rows[:, 1].astype(jnp.float32)
    scores = jnp.einsum('sqhd,skhd->shqk', query_heads, key_heads) * softmax_scale
    weights = jnp.exp(scores - log_part[..., None])
    weight_grad = jnp.einsum('sqhd,skhd->shqk', grad_heads, value_heads)
    score_grad = weights * (weight_grad - delta_part[..., None])
    weights_low = lax.optimization_barrier(weights.astype(jnp.bfloat16)).astype(jnp.float32)
    score_low = lax.optimization_barrier(score_grad.astype(jnp.bfloat16)).astype(jnp.float32)
    value_part = jnp.einsum('shqk,sqhd->skhd', weights_low, grad_heads)
    key_part = jnp.einsum('shqk,sqhd->skhd', score_low, query_heads) * softmax_scale
    query_part = jnp.einsum('shqk,skhd->sqhd', score_low, key_heads) * softmax_scale
    flat_shape = (item_count, block_rows, features)
    return (query_part.reshape(flat_shape), key_part.reshape(flat_shape), value_part.reshape(flat_shape))

def to_blocks(array):
    features = array.shape[-1]
    shaped = array.reshape(N_GX, PX, N_GY, PY, features).transpose(0, 2, 1, 3, 4)
    return shaped.reshape(N_GX, N_GY * RB, BLOCK, features)

def from_blocks(blocks):
    features = blocks.shape[-1]
    shaped = blocks.reshape(N_GX, N_GY, PX, PY, features).transpose(0, 2, 1, 3, 4)
    return shaped.reshape(GRID_X, GRID_Y, features)

def reference(queries, keys, values, out_attn, out_grad, log_norm, neighbour_blocks, stencil):
    features = queries.shape[-1]
    head_width = features // HEADS
    products = out_grad.astype(jnp.float32) * out_attn.astype(jnp.float32)
    delta = products.reshape(GRID_X, GRID_Y, HEADS, head_width).sum(-1).astype(jnp.bfloat16)
    stat_grid = jnp.stack([log_norm, delta.transpose(2, 0, 1)], 0)
    stat_blocks = stat_grid.reshape(2, HEADS, N_GX, PX, N_GY, PY).transpose(2, 4, 0, 1, 3, 5)
    stat_blocks = stat_blocks.reshape(N_GX, N_GY, 2, HEADS, RB, BLOCK).transpose(0, 1, 4, 2, 3, 5)
    stat_blocks = stat_blocks.reshape(N_GX, N_GY * RB, 2, HEADS, BLOCK)
    strip_count = N_GY * RB
    width = NB + 1

    def strip_grads(strip):
        query_strip, key_strip, value_strip, grad_strip, stat_strip, list_strip = strip
        own = jnp.arange(strip_count, dtype=jnp.int32)[:, None]
        chosen = jnp.concatenate([own, list_strip.astype(jnp.int32)], 1)
        flat = chosen.reshape(-1)
        query_part, key_part, value_part = tile_grads(jnp.repeat(query_strip, width, axis=0), jnp.repeat(grad_strip, width, axis=0), jnp.repeat(stat_strip, width, axis=0), key_strip[flat], value_strip[flat], HEADS)
        query_sum = query_part.reshape(strip_count, width, BLOCK, features).sum(1)
        key_sum = jax.ops.segment_sum(key_part, flat, num_segments=strip_count)
        value_sum = jax.ops.segment_sum(value_part, flat, num_segments=strip_count)
        return (query_sum, key_sum, value_sum)
    query_all, key_all, value_all = lax.map(strip_grads, (to_blocks(queries), to_blocks(keys), to_blocks(values), to_blocks(out_grad), stat_blocks, neighbour_blocks))
    grad_float = out_grad.astype(jnp.float32)
    value_float = values.astype(jnp.float32)
    moved = [grad_float, jnp.roll(grad_float, -1, 0), jnp.roll(grad_float, 1, 0), jnp.roll(grad_float, -1, 1), jnp.roll(grad_float, 1, 1)]
    stencil_term = stencil[0] * moved[0]
    for index in range(1, 5):
        stencil_term = stencil_term + stencil[index] * moved[index]
    rows_list = [lax.optimization_barrier(jnp.sum(moved[index] * value_float, axis=(0, 1))) for index in range(5)]
    stencil_grad = jnp.stack(rows_list) / math.sqrt(GRID_X * GRID_Y)
    query_grad = from_blocks(query_all).astype(jnp.bfloat16)
    key_grad = from_blocks(key_all).astype(jnp.bfloat16)
    value_grad = (from_blocks(value_all) + stencil_term).astype(jnp.bfloat16)
    return (query_grad, key_grad, value_grad, stencil_grad)
```

```python
import math

import jax
import jax.numpy as jnp
from jax import lax
from jax.sharding import PartitionSpec as P

BLOCK = 128
HEADS = 4


def with_halo(block, sides, width):
    for axis, dim in sides:
        count = lax.axis_size(axis)
        forward = [(i, i + 1) for i in range(count - 1)]
        forward.append((count - 1, 0))
        backward = [(target, source) for source, target in forward]
        low = lax.ppermute(
            lax.slice_in_dim(block, block.shape[dim] - width, None, axis=dim), axis, forward
        )
        high = lax.ppermute(lax.slice_in_dim(block, 0, width, axis=dim), axis, backward)
        block = jnp.concatenate([low, block, high], axis=dim)
    return block


def prime_factors(count):
    factors = []
    base = 2
    while count > 1:
        while count % base == 0:
            factors.append(base)
            count //= base
        base += 1
    return factors


def exchange_sum(value, axis):
    count = lax.axis_size(axis)
    index = lax.axis_index(axis)
    stride = 1
    for radix in prime_factors(count):
        digit = (index // stride) % radix
        if radix == 2:
            pairs = [(i, i + stride) if (i // stride) % 2 == 0 else (i, i - stride) for i in range(count)]
            value = value + lax.ppermute(value, axis, pairs)
        else:
            received = [value]
            for shift in range(1, radix):
                pairs = []
                for i in range(count):
                    d = (i // stride) % radix
                    pairs.append((i, i + (((d + shift) % radix) - d) * stride))
                received.append(lax.ppermute(value, axis, pairs))
            total = None
            for position in range(radix):
                offset = (digit - position) % radix
                term = received[0]
                for shift in range(1, radix):
                    term = jnp.where(offset == shift, received[shift], term)
                total = term if total is None else total + term
            value = total
        stride *= radix
    return value


def tile_grads(row_pack, stat_pack, key_pack):
    item_count = row_pack.shape[0]
    block_rows = row_pack.shape[2]
    features = row_pack.shape[3]
    head_width = features // HEADS
    softmax_scale = 1.0 / math.sqrt(head_width)
    row_heads = row_pack.reshape(item_count, 2, block_rows, HEADS, head_width).transpose(
        0, 1, 3, 4, 2
    )
    key_heads_all = key_pack.reshape(item_count, 2, block_rows, HEADS, head_width).transpose(
        0, 1, 3, 4, 2
    )
    query_heads = row_heads[:, 0]
    grad_heads = row_heads[:, 1]
    key_heads = key_heads_all[:, 0]
    value_heads = key_heads_all[:, 1]
    log_part = stat_pack[:, 0].astype(jnp.float32)
    delta_part = stat_pack[:, 1].astype(jnp.float32)
    scores = (
        jnp.einsum("shdq,shdk->shqk", query_heads, key_heads, preferred_element_type=jnp.float32)
        * softmax_scale
    )
    weights = jnp.exp(scores - log_part[..., None])
    weight_grad = jnp.einsum(
        "shdq,shdk->shqk", grad_heads, value_heads, preferred_element_type=jnp.float32
    )
    score_grad = weights * (weight_grad - delta_part[..., None])
    weights_low = weights.astype(jnp.bfloat16)
    score_low = score_grad.astype(jnp.bfloat16)
    value_part = jnp.einsum(
        "shqk,shdq->shdk", weights_low, grad_heads, preferred_element_type=jnp.float32
    )
    key_part = (
        jnp.einsum("shqk,shdq->shdk", score_low, query_heads, preferred_element_type=jnp.float32)
        * softmax_scale
    )
    query_part = (
        jnp.einsum("shqk,shdk->shdq", score_low, key_heads, preferred_element_type=jnp.float32)
        * softmax_scale
    )

    def points_last(part):
        return part.reshape(item_count, features, block_rows).transpose(0, 2, 1)

    return (points_last(query_part), points_last(key_part), points_last(value_part))


def per_device(queries, keys, values, out_attn, out_grad, log_norm, neighbour_blocks, stencil):
    tile_x, tile_y, features = queries.shape
    row_blocks = tile_x * tile_y // BLOCK
    head_width = features // HEADS
    listed = neighbour_blocks.shape[2]
    group_size = lax.axis_size("gy")
    pair_count = row_blocks * listed
    capacity = max(2, (pair_count + group_size - 1) // group_size)
    slot_count = group_size * capacity
    query_blocks = queries.reshape(row_blocks, BLOCK, features)
    key_blocks = keys.reshape(row_blocks, BLOCK, features)
    value_blocks = values.reshape(row_blocks, BLOCK, features)
    grad_blocks = out_grad.reshape(row_blocks, BLOCK, features)
    products = out_grad.astype(jnp.float32) * out_attn.astype(jnp.float32)
    delta = products.reshape(row_blocks, BLOCK, HEADS, head_width).sum(-1).astype(jnp.bfloat16)
    delta = delta.transpose(0, 2, 1)
    norm_blocks = log_norm.reshape(HEADS, row_blocks, BLOCK).transpose(1, 0, 2)
    stat_blocks = jnp.stack([norm_blocks, delta], 1)
    row_pack = jnp.stack([query_blocks, grad_blocks], 1)
    key_pack = jnp.stack([key_blocks, value_blocks], 1)
    diag_query, diag_key, diag_value = tile_grads(row_pack, stat_blocks, key_pack)
    columns = neighbour_blocks.reshape(pair_count)
    owners = columns // row_blocks
    inner = columns % row_blocks
    order = jnp.arange(pair_count, dtype=jnp.int32)
    before = (owners[:, None] == owners[None, :]) & (order[None, :] < order[:, None])
    rank = jnp.sum(before.astype(jnp.int32), 1)
    slot_of = owners * capacity + rank
    placed = (jnp.arange(slot_count, dtype=jnp.int32)[:, None] == slot_of[None, :]).astype(
        jnp.float32
    )
    source_rows = (
        (order // listed)[:, None] == jnp.arange(row_blocks, dtype=jnp.int32)[None, :]
    ).astype(jnp.float32)
    picker = jnp.dot(placed, source_rows, precision=lax.Precision.HIGHEST)
    picker_low = picker.astype(jnp.bfloat16)
    send_rows = jnp.dot(
        picker_low, row_pack.reshape(row_blocks, -1), preferred_element_type=jnp.float32
    )
    send_rows = send_rows.astype(jnp.bfloat16).reshape(group_size, capacity, 2, BLOCK, features)
    send_stats = jnp.dot(
        picker_low, stat_blocks.reshape(row_blocks, -1), preferred_element_type=jnp.float32
    )
    send_stats = send_stats.astype(jnp.bfloat16).reshape(group_size, capacity, 2, HEADS, BLOCK)
    send_ids = jnp.dot(placed, (inner + 1).astype(jnp.float32), precision=lax.Precision.HIGHEST)
    send_ids = send_ids.astype(jnp.bfloat16).reshape(group_size, capacity)
    rows_in = lax.all_to_all(send_rows, "gy", split_axis=0, concat_axis=0, tiled=True)
    stats_in = lax.all_to_all(send_stats, "gy", split_axis=0, concat_axis=0, tiled=True)
    ids_in = lax.all_to_all(send_ids, "gy", split_axis=0, concat_axis=0, tiled=True)
    item_count = rows_in.shape[1]
    total_items = group_size * item_count
    wanted = ids_in.astype(jnp.float32).astype(jnp.int32) - 1
    chooser = (wanted[..., None] == jnp.arange(row_blocks, dtype=jnp.int32)).astype(jnp.bfloat16)
    keys_in = jnp.dot(
        chooser.reshape(-1, row_blocks),
        key_pack.reshape(row_blocks, -1),
        preferred_element_type=jnp.float32,
    )
    keys_in = keys_in.astype(jnp.bfloat16).reshape(total_items, 2, BLOCK, features)
    query_part, key_part, value_part = tile_grads(
        rows_in.reshape(total_items, 2, BLOCK, features),
        stats_in.reshape(total_items, 2, HEADS, BLOCK),
        keys_in,
    )
    query_part = query_part.reshape(group_size, item_count, BLOCK, features)
    key_part = key_part.reshape(group_size, item_count, BLOCK, features)
    value_part = value_part.reshape(group_size, item_count, BLOCK, features)
    returned = lax.all_to_all(query_part, "gy", split_axis=0, concat_axis=0, tiled=True)
    returned, pieces, ids_in = (returned, jnp.stack([key_part, value_part], 2), ids_in)
    query_sum = diag_query + jnp.einsum(
        "sr,sbf->rbf",
        picker,
        returned.reshape(slot_count, BLOCK, features),
        precision=lax.Precision.HIGHEST,
    )
    arrived = ids_in.reshape(slot_count).astype(jnp.float32).astype(jnp.int32) - 1
    owned = (arrived[:, None] == jnp.arange(row_blocks, dtype=jnp.int32)[None, :]).astype(
        jnp.float32
    )
    key_value_sum = jnp.einsum(
        "sr,sxbf->rxbf",
        owned,
        pieces.reshape(slot_count, 2, BLOCK, features),
        precision=lax.Precision.HIGHEST,
    )
    key_total = diag_key + key_value_sum[:, 0]
    value_total = diag_value + key_value_sum[:, 1]
    rim = with_halo(out_grad, (("gx", 0), ("gy", 1)), 1)
    moved = [
        out_grad.astype(jnp.float32),
        rim[2:, 1:-1].astype(jnp.float32),
        rim[:-2, 1:-1].astype(jnp.float32),
        rim[1:-1, 2:].astype(jnp.float32),
        rim[1:-1, :-2].astype(jnp.float32),
    ]
    value_float = values.astype(jnp.float32)
    stencil_term = stencil[0] * moved[0]
    for index in range(1, 5):
        stencil_term = stencil_term + stencil[index] * moved[index]
    partial_rows = jnp.stack(
        [jnp.sum(moved[index] * value_float, axis=(0, 1)) for index in range(5)]
    )
    summed = exchange_sum(exchange_sum(partial_rows, "gy"), "gx")
    point_count = tile_x * tile_y * lax.axis_size("gx") * group_size
    stencil_grad = summed / math.sqrt(point_count)
    query_grad = query_sum.reshape(tile_x, tile_y, features).astype(jnp.bfloat16)
    key_grad = key_total.reshape(tile_x, tile_y, features).astype(jnp.bfloat16)
    value_grad = (value_total.reshape(tile_x, tile_y, features) + stencil_term).astype(jnp.bfloat16)
    return (query_grad, key_grad, value_grad, stencil_grad)


def solution(mesh):
    placed = (
        P("gx", "gy", None),
        P("gx", "gy", None),
        P("gx", "gy", None),
        P("gx", "gy", None),
        P("gx", "gy", None),
        P(None, "gx", "gy"),
        P("gx", "gy", None),
        P(),
    )
    return jax.shard_map(
        per_device,
        mesh=mesh,
        in_specs=placed,
        out_specs=(P("gx", "gy", None), P("gx", "gy", None), P("gx", "gy", None), P()),
        check_vma=False,
    )
```

```python
import math

import jax
import jax.numpy as jnp
from jax import lax
from jax.sharding import PartitionSpec as P

BLOCK = 128
HEADS = 4


def with_halo(block, sides, width):
    for axis, dim in sides:
        count = lax.axis_size(axis)
        forward = [(i, i + 1) for i in range(count - 1)]
        forward.append((count - 1, 0))
        backward = [(target, source) for source, target in forward]
        low = lax.ppermute(
            lax.slice_in_dim(block, block.shape[dim] - width, None, axis=dim), axis, forward
        )
        high = lax.ppermute(lax.slice_in_dim(block, 0, width, axis=dim), axis, backward)
        block = jnp.concatenate([low, block, high], axis=dim)
    return block


def prime_factors(count):
    factors = []
    base = 2
    while count > 1:
        while count % base == 0:
            factors.append(base)
            count //= base
        base += 1
    return factors


def exchange_sum(value, axis):
    count = lax.axis_size(axis)
    index = lax.axis_index(axis)
    stride = 1
    for radix in prime_factors(count):
        digit = (index // stride) % radix
        if radix == 2:
            pairs = [(i, i + stride) if (i // stride) % 2 == 0 else (i, i - stride) for i in range(count)]
            value = value + lax.ppermute(value, axis, pairs)
        else:
            received = [value]
            for shift in range(1, radix):
                pairs = []
                for i in range(count):
                    d = (i // stride) % radix
                    pairs.append((i, i + (((d + shift) % radix) - d) * stride))
                received.append(lax.ppermute(value, axis, pairs))
            total = None
            for position in range(radix):
                offset = (digit - position) % radix
                term = received[0]
                for shift in range(1, radix):
                    term = jnp.where(offset == shift, received[shift], term)
                total = term if total is None else total + term
            value = total
        stride *= radix
    return value


def tile_grads(row_pack, stat_pack, key_pack):
    item_count = row_pack.shape[0]
    block_rows = row_pack.shape[2]
    features = row_pack.shape[3]
    head_width = features // HEADS
    softmax_scale = 1.0 / math.sqrt(head_width)
    row_heads = row_pack.reshape(item_count, 2, block_rows, HEADS, head_width).transpose(
        0, 1, 3, 4, 2
    )
    key_heads_all = key_pack.reshape(item_count, 2, block_rows, HEADS, head_width).transpose(
        0, 1, 3, 4, 2
    )
    query_heads = row_heads[:, 0]
    grad_heads = row_heads[:, 1]
    key_heads = key_heads_all[:, 0]
    value_heads = key_heads_all[:, 1]
    log_part = stat_pack[:, 0].astype(jnp.float32)
    delta_part = stat_pack[:, 1].astype(jnp.float32)
    scores = (
        jnp.einsum("shdq,shdk->shqk", query_heads, key_heads, preferred_element_type=jnp.float32)
        * softmax_scale
    )
    weights = jnp.exp(scores - log_part[..., None])
    weight_grad = jnp.einsum(
        "shdq,shdk->shqk", grad_heads, value_heads, preferred_element_type=jnp.float32
    )
    score_grad = weights * (weight_grad - delta_part[..., None])
    weights_low = weights.astype(jnp.bfloat16)
    score_low = score_grad.astype(jnp.bfloat16)
    value_part = jnp.einsum(
        "shqk,shdq->shdk", weights_low, grad_heads, preferred_element_type=jnp.float32
    )
    key_part = (
        jnp.einsum("shqk,shdq->shdk", score_low, query_heads, preferred_element_type=jnp.float32)
        * softmax_scale
    )
    query_part = (
        jnp.einsum("shqk,shdk->shdq", score_low, key_heads, preferred_element_type=jnp.float32)
        * softmax_scale
    )

    def points_last(part):
        return part.reshape(item_count, features, block_rows).transpose(0, 2, 1)

    return (points_last(query_part), points_last(key_part), points_last(value_part))


def per_device(queries, keys, values, out_attn, out_grad, log_norm, neighbour_blocks, stencil):
    tile_x, tile_y, features = queries.shape
    row_blocks = tile_x * tile_y // BLOCK
    head_width = features // HEADS
    listed = neighbour_blocks.shape[2]
    group_size = lax.axis_size("gy")
    pair_count = row_blocks * listed
    capacity = max(2, (pair_count + group_size - 1) // group_size)
    slot_count = group_size * capacity
    query_blocks = queries.reshape(row_blocks, BLOCK, features)
    key_blocks = keys.reshape(row_blocks, BLOCK, features)
    value_blocks = values.reshape(row_blocks, BLOCK, features)
    grad_blocks = out_grad.reshape(row_blocks, BLOCK, features)
    products = out_grad.astype(jnp.float32) * out_attn.astype(jnp.float32)
    delta = products.reshape(row_blocks, BLOCK, HEADS, head_width).sum(-1).astype(jnp.bfloat16)
    delta = delta.transpose(0, 2, 1)
    norm_blocks = log_norm.reshape(HEADS, row_blocks, BLOCK).transpose(1, 0, 2)
    stat_blocks = jnp.stack([norm_blocks, delta], 1)
    row_pack = jnp.stack([query_blocks, grad_blocks], 1)
    key_pack = jnp.stack([key_blocks, value_blocks], 1)
    diag_query, diag_key, diag_value = tile_grads(row_pack, stat_blocks, key_pack)
    columns = neighbour_blocks.reshape(pair_count)
    owners = columns // row_blocks
    inner = columns % row_blocks
    order = jnp.arange(pair_count, dtype=jnp.int32)
    before = (owners[:, None] == owners[None, :]) & (order[None, :] < order[:, None])
    rank = jnp.sum(before.astype(jnp.int32), 1)
    slot_of = owners * capacity + rank
    placed = (jnp.arange(slot_count, dtype=jnp.int32)[:, None] == slot_of[None, :]).astype(
        jnp.float32
    )
    source_rows = (
        (order // listed)[:, None] == jnp.arange(row_blocks, dtype=jnp.int32)[None, :]
    ).astype(jnp.float32)
    picker = jnp.dot(placed, source_rows, precision=lax.Precision.HIGHEST)
    picker_low = picker.astype(jnp.bfloat16)
    send_rows = jnp.dot(
        picker_low, row_pack.reshape(row_blocks, -1), preferred_element_type=jnp.float32
    )
    send_rows = send_rows.astype(jnp.bfloat16).reshape(group_size, capacity, 2, BLOCK, features)
    send_stats = jnp.dot(
        picker_low, stat_blocks.reshape(row_blocks, -1), preferred_element_type=jnp.float32
    )
    send_stats = send_stats.astype(jnp.bfloat16).reshape(group_size, capacity, 2, HEADS, BLOCK)
    send_ids = jnp.dot(placed, (inner + 1).astype(jnp.float32), precision=lax.Precision.HIGHEST)
    send_ids = send_ids.astype(jnp.bfloat16).reshape(group_size, capacity)
    rows_in = lax.all_to_all(send_rows, "gy", split_axis=0, concat_axis=0, tiled=True)
    stats_in = lax.all_to_all(send_stats, "gy", split_axis=0, concat_axis=0, tiled=True)
    ids_in = lax.all_to_all(send_ids, "gy", split_axis=0, concat_axis=0, tiled=True)
    item_count = rows_in.shape[1]
    total_items = group_size * item_count
    wanted = ids_in.astype(jnp.float32).astype(jnp.int32) - 1
    chooser = (wanted[..., None] == jnp.arange(row_blocks, dtype=jnp.int32)).astype(jnp.bfloat16)
    keys_in = jnp.dot(
        chooser.reshape(-1, row_blocks),
        key_pack.reshape(row_blocks, -1),
        preferred_element_type=jnp.float32,
    )
    keys_in = keys_in.astype(jnp.bfloat16).reshape(total_items, 2, BLOCK, features)
    query_part, key_part, value_part = tile_grads(
        rows_in.reshape(total_items, 2, BLOCK, features),
        stats_in.reshape(total_items, 2, HEADS, BLOCK),
        keys_in,
    )
    query_part = query_part.reshape(group_size, item_count, BLOCK, features)
    key_part = key_part.reshape(group_size, item_count, BLOCK, features)
    value_part = value_part.reshape(group_size, item_count, BLOCK, features)
    returned = lax.all_to_all(query_part, "gy", split_axis=0, concat_axis=0, tiled=True)
    returned, pieces, ids_in = (returned, jnp.stack([key_part, value_part], 2), ids_in)
    query_sum = diag_query + jnp.einsum(
        "sr,sbf->rbf",
        picker,
        returned.reshape(slot_count, BLOCK, features),
        precision=lax.Precision.HIGHEST,
    )
    arrived = ids_in.reshape(slot_count).astype(jnp.float32).astype(jnp.int32) - 1
    owned = (arrived[:, None] == jnp.arange(row_blocks, dtype=jnp.int32)[None, :]).astype(
        jnp.float32
    )
    key_value_sum = jnp.einsum(
        "sr,sxbf->rxbf",
        owned,
        pieces.reshape(slot_count, 2, BLOCK, features),
        precision=lax.Precision.HIGHEST,
    )
    key_total = diag_key + key_value_sum[:, 0]
    value_total = diag_value + key_value_sum[:, 1]
    rim = with_halo(out_grad, (("gx", 0), ("gy", 1)), 1)
    moved = [
        out_grad.astype(jnp.float32),
        rim[2:, 1:-1].astype(jnp.float32),
        rim[:-2, 1:-1].astype(jnp.float32),
        rim[1:-1, 2:].astype(jnp.float32),
        rim[1:-1, :-2].astype(jnp.float32),
    ]
    value_float = values.astype(jnp.float32)
    stencil_term = stencil[0] * moved[0]
    for index in range(1, 5):
        stencil_term = stencil_term + stencil[index] * moved[index]
    partial_rows = jnp.stack(
        [jnp.sum(moved[index] * value_float, axis=(0, 1)) for index in range(5)]
    )
    gathered = lax.all_gather(partial_rows, ("gx", "gy"), tiled=False)
    summed = jnp.sum(gathered, axis=0)
    point_count = tile_x * tile_y * lax.axis_size("gx") * group_size
    stencil_grad = summed / math.sqrt(point_count)
    query_grad = query_sum.reshape(tile_x, tile_y, features).astype(jnp.bfloat16)
    key_grad = key_total.reshape(tile_x, tile_y, features).astype(jnp.bfloat16)
    value_grad = (value_total.reshape(tile_x, tile_y, features) + stencil_term).astype(jnp.bfloat16)
    return (query_grad, key_grad, value_grad, stencil_grad)


def solution(mesh):
    placed = (
        P("gx", "gy", None),
        P("gx", "gy", None),
        P("gx", "gy", None),
        P("gx", "gy", None),
        P("gx", "gy", None),
        P(None, "gx", "gy"),
        P("gx", "gy", None),
        P(),
    )
    return jax.shard_map(
        per_device,
        mesh=mesh,
        in_specs=placed,
        out_specs=(P("gx", "gy", None), P("gx", "gy", None), P("gx", "gy", None), P()),
        check_vma=False,
    )
```

```python
import math

import jax
import jax.numpy as jnp
from jax import lax
from jax.sharding import PartitionSpec as P

BLOCK = 128
HEADS = 4


def with_halo(block, sides, width):
    for axis, dim in sides:
        count = lax.axis_size(axis)
        forward = [(i, i + 1) for i in range(count - 1)]
        forward.append((count - 1, 0))
        backward = [(target, source) for source, target in forward]
        low = lax.ppermute(
            lax.slice_in_dim(block, block.shape[dim] - width, None, axis=dim), axis, forward
        )
        high = lax.ppermute(lax.slice_in_dim(block, 0, width, axis=dim), axis, backward)
        block = jnp.concatenate([low, block, high], axis=dim)
    return block


def prime_factors(count):
    factors = []
    base = 2
    while count > 1:
        while count % base == 0:
            factors.append(base)
            count //= base
        base += 1
    return factors


def exchange_sum(value, axis):
    count = lax.axis_size(axis)
    index = lax.axis_index(axis)
    stride = 1
    for radix in prime_factors(count):
        digit = (index // stride) % radix
        if radix == 2:
            pairs = [(i, i + stride) if (i // stride) % 2 == 0 else (i, i - stride) for i in range(count)]
            value = value + lax.ppermute(value, axis, pairs)
        else:
            received = [value]
            for shift in range(1, radix):
                pairs = []
                for i in range(count):
                    d = (i // stride) % radix
                    pairs.append((i, i + (((d + shift) % radix) - d) * stride))
                received.append(lax.ppermute(value, axis, pairs))
            total = None
            for position in range(radix):
                offset = (digit - position) % radix
                term = received[0]
                for shift in range(1, radix):
                    term = jnp.where(offset == shift, received[shift], term)
                total = term if total is None else total + term
            value = total
        stride *= radix
    return value


def gather_sum(value, axis):
    count = lax.axis_size(axis)
    spread = jnp.broadcast_to(value[None], (count,) + value.shape)
    parts = lax.all_to_all(spread, axis, split_axis=0, concat_axis=0, tiled=True)
    return jnp.sum(parts, axis=0)


def tile_grads(row_pack, stat_pack, key_pack):
    item_count = row_pack.shape[0]
    block_rows = row_pack.shape[2]
    features = row_pack.shape[3]
    head_width = features // HEADS
    softmax_scale = 1.0 / math.sqrt(head_width)
    row_heads = row_pack.reshape(item_count, 2, block_rows, HEADS, head_width).transpose(
        0, 1, 3, 4, 2
    )
    key_heads_all = key_pack.reshape(item_count, 2, block_rows, HEADS, head_width).transpose(
        0, 1, 3, 4, 2
    )
    query_heads = row_heads[:, 0]
    grad_heads = row_heads[:, 1]
    key_heads = key_heads_all[:, 0]
    value_heads = key_heads_all[:, 1]
    log_part = stat_pack[:, 0].astype(jnp.float32)
    delta_part = stat_pack[:, 1].astype(jnp.float32)
    scores = (
        jnp.einsum("shdq,shdk->shqk", query_heads, key_heads, preferred_element_type=jnp.float32)
        * softmax_scale
    )
    weights = jnp.exp(scores - log_part[..., None])
    weight_grad = jnp.einsum(
        "shdq,shdk->shqk", grad_heads, value_heads, preferred_element_type=jnp.float32
    )
    score_grad = weights * (weight_grad - delta_part[..., None])
    weights_low = weights.astype(jnp.bfloat16)
    score_low = score_grad.astype(jnp.bfloat16)
    value_part = jnp.einsum(
        "shqk,shdq->shdk", weights_low, grad_heads, preferred_element_type=jnp.float32
    )
    key_part = (
        jnp.einsum("shqk,shdq->shdk", score_low, query_heads, preferred_element_type=jnp.float32)
        * softmax_scale
    )
    query_part = (
        jnp.einsum("shqk,shdk->shdq", score_low, key_heads, preferred_element_type=jnp.float32)
        * softmax_scale
    )

    def points_last(part):
        return part.reshape(item_count, features, block_rows).transpose(0, 2, 1)

    return (points_last(query_part), points_last(key_part), points_last(value_part))


def per_device(queries, keys, values, out_attn, out_grad, log_norm, neighbour_blocks, stencil):
    tile_x, tile_y, features = queries.shape
    row_blocks = tile_x * tile_y // BLOCK
    head_width = features // HEADS
    listed = neighbour_blocks.shape[2]
    group_size = lax.axis_size("gy")
    pair_count = row_blocks * listed
    capacity = max(2, (pair_count + group_size - 1) // group_size)
    slot_count = group_size * capacity
    query_blocks = queries.reshape(row_blocks, BLOCK, features)
    key_blocks = keys.reshape(row_blocks, BLOCK, features)
    value_blocks = values.reshape(row_blocks, BLOCK, features)
    grad_blocks = out_grad.reshape(row_blocks, BLOCK, features)
    products = out_grad.astype(jnp.float32) * out_attn.astype(jnp.float32)
    delta = products.reshape(row_blocks, BLOCK, HEADS, head_width).sum(-1).astype(jnp.bfloat16)
    delta = delta.transpose(0, 2, 1)
    norm_blocks = log_norm.reshape(HEADS, row_blocks, BLOCK).transpose(1, 0, 2)
    stat_blocks = jnp.stack([norm_blocks, delta], 1)
    row_pack = jnp.stack([query_blocks, grad_blocks], 1)
    key_pack = jnp.stack([key_blocks, value_blocks], 1)
    diag_query, diag_key, diag_value = tile_grads(row_pack, stat_blocks, key_pack)
    columns = neighbour_blocks.reshape(pair_count)
    owners = columns // row_blocks
    inner = columns % row_blocks
    order = jnp.arange(pair_count, dtype=jnp.int32)
    before = (owners[:, None] == owners[None, :]) & (order[None, :] < order[:, None])
    rank = jnp.sum(before.astype(jnp.int32), 1)
    slot_of = owners * capacity + rank
    placed = (jnp.arange(slot_count, dtype=jnp.int32)[:, None] == slot_of[None, :]).astype(
        jnp.float32
    )
    source_rows = (
        (order // listed)[:, None] == jnp.arange(row_blocks, dtype=jnp.int32)[None, :]
    ).astype(jnp.float32)
    picker = jnp.dot(placed, source_rows, precision=lax.Precision.HIGHEST)
    picker_low = picker.astype(jnp.bfloat16)
    send_rows = jnp.dot(
        picker_low, row_pack.reshape(row_blocks, -1), preferred_element_type=jnp.float32
    )
    send_rows = send_rows.astype(jnp.bfloat16).reshape(group_size, capacity, 2, BLOCK, features)
    send_stats = jnp.dot(
        picker_low, stat_blocks.reshape(row_blocks, -1), preferred_element_type=jnp.float32
    )
    send_stats = send_stats.astype(jnp.bfloat16).reshape(group_size, capacity, 2, HEADS, BLOCK)
    send_ids = jnp.dot(placed, (inner + 1).astype(jnp.float32), precision=lax.Precision.HIGHEST)
    send_ids = send_ids.astype(jnp.bfloat16).reshape(group_size, capacity)
    rows_in = lax.all_to_all(send_rows, "gy", split_axis=0, concat_axis=0, tiled=True)
    stats_in = lax.all_to_all(send_stats, "gy", split_axis=0, concat_axis=0, tiled=True)
    ids_in = lax.all_to_all(send_ids, "gy", split_axis=0, concat_axis=0, tiled=True)
    item_count = rows_in.shape[1]
    total_items = group_size * item_count
    wanted = ids_in.astype(jnp.float32).astype(jnp.int32) - 1
    chooser = (wanted[..., None] == jnp.arange(row_blocks, dtype=jnp.int32)).astype(jnp.bfloat16)
    keys_in = jnp.dot(
        chooser.reshape(-1, row_blocks),
        key_pack.reshape(row_blocks, -1),
        preferred_element_type=jnp.float32,
    )
    keys_in = keys_in.astype(jnp.bfloat16).reshape(total_items, 2, BLOCK, features)
    query_part, key_part, value_part = tile_grads(
        rows_in.reshape(total_items, 2, BLOCK, features),
        stats_in.reshape(total_items, 2, HEADS, BLOCK),
        keys_in,
    )
    query_part = query_part.reshape(group_size, item_count, BLOCK, features)
    key_part = key_part.reshape(group_size, item_count, BLOCK, features)
    value_part = value_part.reshape(group_size, item_count, BLOCK, features)
    returned = lax.all_to_all(query_part, "gy", split_axis=0, concat_axis=0, tiled=True)
    returned, pieces, ids_in = (returned, jnp.stack([key_part, value_part], 2), ids_in)
    query_sum = diag_query + jnp.einsum(
        "sr,sbf->rbf",
        picker,
        returned.reshape(slot_count, BLOCK, features),
        precision=lax.Precision.HIGHEST,
    )
    arrived = ids_in.reshape(slot_count).astype(jnp.float32).astype(jnp.int32) - 1
    owned = (arrived[:, None] == jnp.arange(row_blocks, dtype=jnp.int32)[None, :]).astype(
        jnp.float32
    )
    key_value_sum = jnp.einsum(
        "sr,sxbf->rxbf",
        owned,
        pieces.reshape(slot_count, 2, BLOCK, features),
        precision=lax.Precision.HIGHEST,
    )
    key_total = diag_key + key_value_sum[:, 0]
    value_total = diag_value + key_value_sum[:, 1]
    rim = with_halo(out_grad, (("gx", 0), ("gy", 1)), 1)
    moved = [
        out_grad.astype(jnp.float32),
        rim[2:, 1:-1].astype(jnp.float32),
        rim[:-2, 1:-1].astype(jnp.float32),
        rim[1:-1, 2:].astype(jnp.float32),
        rim[1:-1, :-2].astype(jnp.float32),
    ]
    value_float = values.astype(jnp.float32)
    stencil_term = stencil[0] * moved[0]
    for index in range(1, 5):
        stencil_term = stencil_term + stencil[index] * moved[index]
    partial_rows = jnp.stack(
        [jnp.sum(moved[index] * value_float, axis=(0, 1)) for index in range(5)]
    )
    summed = gather_sum(gather_sum(partial_rows, "gy"), "gx")
    point_count = tile_x * tile_y * lax.axis_size("gx") * group_size
    stencil_grad = summed / math.sqrt(point_count)
    query_grad = query_sum.reshape(tile_x, tile_y, features).astype(jnp.bfloat16)
    key_grad = key_total.reshape(tile_x, tile_y, features).astype(jnp.bfloat16)
    value_grad = (value_total.reshape(tile_x, tile_y, features) + stencil_term).astype(jnp.bfloat16)
    return (query_grad, key_grad, value_grad, stencil_grad)


def solution(mesh):
    placed = (
        P("gx", "gy", None),
        P("gx", "gy", None),
        P("gx", "gy", None),
        P("gx", "gy", None),
        P("gx", "gy", None),
        P(None, "gx", "gy"),
        P("gx", "gy", None),
        P(),
    )
    return jax.shard_map(
        per_device,
        mesh=mesh,
        in_specs=placed,
        out_specs=(P("gx", "gy", None), P("gx", "gy", None), P("gx", "gy", None), P()),
        check_vma=False,
    )
```

```python
import math

import jax
import jax.numpy as jnp
from jax import lax
from jax.sharding import PartitionSpec as P

BLOCK = 128
HEADS = 4


def with_halo(block, sides, width):
    for axis, dim in sides:
        count = lax.axis_size(axis)
        forward = [(i, i + 1) for i in range(count - 1)]
        forward.append((count - 1, 0))
        backward = [(target, source) for source, target in forward]
        low = lax.ppermute(
            lax.slice_in_dim(block, block.shape[dim] - width, None, axis=dim), axis, forward
        )
        high = lax.ppermute(lax.slice_in_dim(block, 0, width, axis=dim), axis, backward)
        block = jnp.concatenate([low, block, high], axis=dim)
    return block


def prime_factors(count):
    factors = []
    base = 2
    while count > 1:
        while count % base == 0:
            factors.append(base)
            count //= base
        base += 1
    return factors


def exchange_sum(value, axis):
    count = lax.axis_size(axis)
    index = lax.axis_index(axis)
    stride = 1
    for radix in prime_factors(count):
        digit = (index // stride) % radix
        if radix == 2:
            pairs = [(i, i + stride) if (i // stride) % 2 == 0 else (i, i - stride) for i in range(count)]
            value = value + lax.ppermute(value, axis, pairs)
        else:
            received = [value]
            for shift in range(1, radix):
                pairs = []
                for i in range(count):
                    d = (i // stride) % radix
                    pairs.append((i, i + (((d + shift) % radix) - d) * stride))
                received.append(lax.ppermute(value, axis, pairs))
            total = None
            for position in range(radix):
                offset = (digit - position) % radix
                term = received[0]
                for shift in range(1, radix):
                    term = jnp.where(offset == shift, received[shift], term)
                total = term if total is None else total + term
            value = total
        stride *= radix
    return value


def gather_sum(value, axis):
    count = lax.axis_size(axis)
    spread = jnp.broadcast_to(value[None], (count,) + value.shape)
    parts = lax.all_to_all(spread, axis, split_axis=0, concat_axis=0, tiled=True)
    return jnp.sum(parts, axis=0)


def tile_grads(row_pack, stat_pack, key_pack):
    item_count = row_pack.shape[0]
    block_rows = row_pack.shape[2]
    features = row_pack.shape[3]
    head_width = features // HEADS
    softmax_scale = 1.0 / math.sqrt(head_width)
    row_heads = row_pack.reshape(item_count, 2, block_rows, HEADS, head_width).transpose(
        0, 1, 3, 4, 2
    )
    key_heads_all = key_pack.reshape(item_count, 2, block_rows, HEADS, head_width).transpose(
        0, 1, 3, 4, 2
    )
    query_heads = row_heads[:, 0]
    grad_heads = row_heads[:, 1]
    key_heads = key_heads_all[:, 0]
    value_heads = key_heads_all[:, 1]
    log_part = stat_pack[:, 0].astype(jnp.float32)
    delta_part = stat_pack[:, 1].astype(jnp.float32)
    scores = (
        jnp.einsum("shdq,shdk->shqk", query_heads, key_heads, preferred_element_type=jnp.float32)
        * softmax_scale
    )
    weights = jnp.exp(scores - log_part[..., None])
    weight_grad = jnp.einsum(
        "shdq,shdk->shqk", grad_heads, value_heads, preferred_element_type=jnp.float32
    )
    score_grad = weights * (weight_grad - delta_part[..., None])
    weights_low = weights.astype(jnp.bfloat16)
    score_low = score_grad.astype(jnp.bfloat16)
    value_part = jnp.einsum(
        "shqk,shdq->shdk", weights_low, grad_heads, preferred_element_type=jnp.float32
    )
    key_part = (
        jnp.einsum("shqk,shdq->shdk", score_low, query_heads, preferred_element_type=jnp.float32)
        * softmax_scale
    )
    query_part = (
        jnp.einsum("shqk,shdk->shdq", score_low, key_heads, preferred_element_type=jnp.float32)
        * softmax_scale
    )

    def points_last(part):
        return part.reshape(item_count, features, block_rows).transpose(0, 2, 1)

    return (points_last(query_part), points_last(key_part), points_last(value_part))


def per_device(queries, keys, values, out_attn, out_grad, log_norm, neighbour_blocks, stencil):
    tile_x, tile_y, features = queries.shape
    row_blocks = tile_x * tile_y // BLOCK
    head_width = features // HEADS
    listed = neighbour_blocks.shape[2]
    group_size = lax.axis_size("gy")
    pair_count = row_blocks * listed
    capacity = max(2, (pair_count + group_size - 1) // group_size)
    slot_count = group_size * capacity
    query_blocks = queries.reshape(row_blocks, BLOCK, features)
    key_blocks = keys.reshape(row_blocks, BLOCK, features)
    value_blocks = values.reshape(row_blocks, BLOCK, features)
    grad_blocks = out_grad.reshape(row_blocks, BLOCK, features)
    products = out_grad.astype(jnp.float32) * out_attn.astype(jnp.float32)
    delta = products.reshape(row_blocks, BLOCK, HEADS, head_width).sum(-1).astype(jnp.bfloat16)
    delta = delta.transpose(0, 2, 1)
    norm_blocks = log_norm.reshape(HEADS, row_blocks, BLOCK).transpose(1, 0, 2)
    stat_blocks = jnp.stack([norm_blocks, delta], 1)
    row_pack = jnp.stack([query_blocks, grad_blocks], 1)
    key_pack = jnp.stack([key_blocks, value_blocks], 1)
    diag_query, diag_key, diag_value = tile_grads(row_pack, stat_blocks, key_pack)
    rim = with_halo(out_grad, (("gx", 0), ("gy", 1)), 1)
    moved = [
        out_grad.astype(jnp.float32),
        rim[2:, 1:-1].astype(jnp.float32),
        rim[:-2, 1:-1].astype(jnp.float32),
        rim[1:-1, 2:].astype(jnp.float32),
        rim[1:-1, :-2].astype(jnp.float32),
    ]
    value_float = values.astype(jnp.float32)
    stencil_term = stencil[0] * moved[0]
    for index in range(1, 5):
        stencil_term = stencil_term + stencil[index] * moved[index]
    partial_rows = jnp.stack(
        [jnp.sum(moved[index] * value_float, axis=(0, 1)) for index in range(5)]
    )
    column_sum = gather_sum(partial_rows, "gx")
    point_count = tile_x * tile_y * lax.axis_size("gx") * group_size
    columns = neighbour_blocks.reshape(pair_count)
    owners = columns // row_blocks
    inner = columns % row_blocks
    order = jnp.arange(pair_count, dtype=jnp.int32)
    before = (owners[:, None] == owners[None, :]) & (order[None, :] < order[:, None])
    rank = jnp.sum(before.astype(jnp.int32), 1)
    slot_of = owners * capacity + rank
    placed = (jnp.arange(slot_count, dtype=jnp.int32)[:, None] == slot_of[None, :]).astype(
        jnp.float32
    )
    source_rows = (
        (order // listed)[:, None] == jnp.arange(row_blocks, dtype=jnp.int32)[None, :]
    ).astype(jnp.float32)
    picker = jnp.dot(placed, source_rows, precision=lax.Precision.HIGHEST)
    picker_low = picker.astype(jnp.bfloat16)
    send_rows = jnp.dot(
        picker_low, row_pack.reshape(row_blocks, -1), preferred_element_type=jnp.float32
    )
    send_rows = send_rows.astype(jnp.bfloat16).reshape(group_size, capacity, 2, BLOCK, features)
    send_stats = jnp.dot(
        picker_low, stat_blocks.reshape(row_blocks, -1), preferred_element_type=jnp.float32
    )
    send_stats = send_stats.astype(jnp.bfloat16).reshape(group_size, capacity, 2, HEADS, BLOCK)
    send_ids = jnp.dot(placed, (inner + 1).astype(jnp.float32), precision=lax.Precision.HIGHEST)
    send_ids = send_ids.astype(jnp.bfloat16).reshape(group_size, capacity)
    stat_rows = send_stats.reshape(group_size, capacity, 2 * HEADS, BLOCK)
    id_rows = jnp.broadcast_to(send_ids[:, :, None, None], (group_size, capacity, 8, features))
    row_count = 2 * BLOCK
    send_pack = jnp.concatenate(
        [send_rows.reshape(group_size, capacity, row_count, features), stat_rows, id_rows], 2
    )
    pack_in = lax.all_to_all(send_pack, "gy", split_axis=0, concat_axis=0, tiled=True)
    rows_in = pack_in[:, :, :row_count].reshape(group_size, capacity, 2, BLOCK, features)
    stats_in = pack_in[:, :, row_count : row_count + 2 * HEADS].reshape(
        group_size, capacity, 2, HEADS, BLOCK
    )
    ids_in = pack_in[:, :, row_count + 2 * HEADS, 0]
    item_count = rows_in.shape[1]
    total_items = group_size * item_count
    wanted = ids_in.astype(jnp.float32).astype(jnp.int32) - 1
    chooser = (wanted[..., None] == jnp.arange(row_blocks, dtype=jnp.int32)).astype(jnp.bfloat16)
    keys_in = jnp.dot(
        chooser.reshape(-1, row_blocks),
        key_pack.reshape(row_blocks, -1),
        preferred_element_type=jnp.float32,
    )
    keys_in = keys_in.astype(jnp.bfloat16).reshape(total_items, 2, BLOCK, features)
    query_part, key_part, value_part = tile_grads(
        rows_in.reshape(total_items, 2, BLOCK, features),
        stats_in.reshape(total_items, 2, HEADS, BLOCK),
        keys_in,
    )
    query_part = query_part.reshape(group_size, item_count, BLOCK, features)
    key_part = key_part.reshape(group_size, item_count, BLOCK, features)
    value_part = value_part.reshape(group_size, item_count, BLOCK, features)
    stencil_count = partial_rows.shape[0]
    stencil_pad = jnp.pad(column_sum, ((0, 8 - stencil_count), (0, 0)))
    return_pack = jnp.concatenate(
        [
            query_part.reshape(group_size, item_count * BLOCK, features),
            jnp.broadcast_to(stencil_pad[None], (group_size, 8, features)),
        ],
        1,
    )
    return_in = lax.all_to_all(return_pack, "gy", split_axis=0, concat_axis=0, tiled=True)
    returned = return_in[:, : item_count * BLOCK]
    summed = jnp.sum(return_in[:, item_count * BLOCK : item_count * BLOCK + stencil_count], 0)
    returned, pieces, ids_in = (returned, jnp.stack([key_part, value_part], 2), ids_in)
    query_sum = diag_query + jnp.einsum(
        "sr,sbf->rbf",
        picker,
        returned.reshape(slot_count, BLOCK, features),
        precision=lax.Precision.HIGHEST,
    )
    arrived = ids_in.reshape(slot_count).astype(jnp.float32).astype(jnp.int32) - 1
    owned = (arrived[:, None] == jnp.arange(row_blocks, dtype=jnp.int32)[None, :]).astype(
        jnp.float32
    )
    key_value_sum = jnp.einsum(
        "sr,sxbf->rxbf",
        owned,
        pieces.reshape(slot_count, 2, BLOCK, features),
        precision=lax.Precision.HIGHEST,
    )
    key_total = diag_key + key_value_sum[:, 0]
    value_total = diag_value + key_value_sum[:, 1]
    stencil_grad = summed / math.sqrt(point_count)
    query_grad = query_sum.reshape(tile_x, tile_y, features).astype(jnp.bfloat16)
    key_grad = key_total.reshape(tile_x, tile_y, features).astype(jnp.bfloat16)
    value_grad = (value_total.reshape(tile_x, tile_y, features) + stencil_term).astype(jnp.bfloat16)
    return (query_grad, key_grad, value_grad, stencil_grad)


def solution(mesh):
    placed = (
        P("gx", "gy", None),
        P("gx", "gy", None),
        P("gx", "gy", None),
        P("gx", "gy", None),
        P("gx", "gy", None),
        P(None, "gx", "gy"),
        P("gx", "gy", None),
        P(),
    )
    return jax.shard_map(
        per_device,
        mesh=mesh,
        in_specs=placed,
        out_specs=(P("gx", "gy", None), P("gx", "gy", None), P("gx", "gy", None), P()),
        check_vma=False,
    )
```

```python
import math

import jax
import jax.numpy as jnp
from jax import lax
from jax.sharding import PartitionSpec as P

BLOCK = 128
HEADS = 4


def with_halo(block, sides, width):
    for axis, dim in sides:
        count = lax.axis_size(axis)
        forward = [(i, i + 1) for i in range(count - 1)]
        forward.append((count - 1, 0))
        backward = [(target, source) for source, target in forward]
        low = lax.ppermute(
            lax.slice_in_dim(block, block.shape[dim] - width, None, axis=dim), axis, forward
        )
        high = lax.ppermute(lax.slice_in_dim(block, 0, width, axis=dim), axis, backward)
        block = jnp.concatenate([low, block, high], axis=dim)
    return block


def prime_factors(count):
    factors = []
    base = 2
    while count > 1:
        while count % base == 0:
            factors.append(base)
            count //= base
        base += 1
    return factors


def exchange_sum(value, axis):
    count = lax.axis_size(axis)
    index = lax.axis_index(axis)
    stride = 1
    for radix in prime_factors(count):
        digit = (index // stride) % radix
        if radix == 2:
            pairs = [(i, i + stride) if (i // stride) % 2 == 0 else (i, i - stride) for i in range(count)]
            value = value + lax.ppermute(value, axis, pairs)
        else:
            received = [value]
            for shift in range(1, radix):
                pairs = []
                for i in range(count):
                    d = (i // stride) % radix
                    pairs.append((i, i + (((d + shift) % radix) - d) * stride))
                received.append(lax.ppermute(value, axis, pairs))
            total = None
            for position in range(radix):
                offset = (digit - position) % radix
                term = received[0]
                for shift in range(1, radix):
                    term = jnp.where(offset == shift, received[shift], term)
                total = term if total is None else total + term
            value = total
        stride *= radix
    return value


def gather_sum(value, axis):
    count = lax.axis_size(axis)
    spread = jnp.broadcast_to(value[None], (count,) + value.shape)
    parts = lax.all_to_all(spread, axis, split_axis=0, concat_axis=0, tiled=True)
    return jnp.sum(parts, axis=0)


def tile_grads(row_pack, stat_pack, key_pack):
    item_count = row_pack.shape[0]
    block_rows = row_pack.shape[2]
    features = row_pack.shape[3]
    head_width = features // HEADS
    softmax_scale = 1.0 / math.sqrt(head_width)
    row_heads = row_pack.reshape(item_count, 2, block_rows, HEADS, head_width).transpose(
        0, 1, 3, 4, 2
    )
    key_heads_all = key_pack.reshape(item_count, 2, block_rows, HEADS, head_width).transpose(
        0, 1, 3, 4, 2
    )
    query_heads = row_heads[:, 0]
    grad_heads = row_heads[:, 1]
    key_heads = key_heads_all[:, 0]
    value_heads = key_heads_all[:, 1]
    log_part = stat_pack[:, 0].astype(jnp.float32)
    delta_part = stat_pack[:, 1].astype(jnp.float32)
    scores = (
        jnp.einsum("shdq,shdk->shqk", query_heads, key_heads, preferred_element_type=jnp.float32)
        * softmax_scale
    )
    weights = jnp.exp(scores - log_part[..., None])
    weight_grad = jnp.einsum(
        "shdq,shdk->shqk", grad_heads, value_heads, preferred_element_type=jnp.float32
    )
    score_grad = weights * (weight_grad - delta_part[..., None])
    weights_low = weights.astype(jnp.bfloat16)
    score_low = score_grad.astype(jnp.bfloat16)
    value_part = jnp.einsum(
        "shqk,shdq->shdk", weights_low, grad_heads, preferred_element_type=jnp.float32
    )
    key_part = (
        jnp.einsum("shqk,shdq->shdk", score_low, query_heads, preferred_element_type=jnp.float32)
        * softmax_scale
    )
    query_part = (
        jnp.einsum("shqk,shdk->shdq", score_low, key_heads, preferred_element_type=jnp.float32)
        * softmax_scale
    )

    def points_last(part):
        return part.reshape(item_count, features, block_rows).transpose(0, 2, 1)

    return (points_last(query_part), points_last(key_part), points_last(value_part))


def per_device(queries, keys, values, out_attn, out_grad, log_norm, neighbour_blocks, stencil):
    tile_x, tile_y, features = queries.shape
    row_blocks = tile_x * tile_y // BLOCK
    head_width = features // HEADS
    listed = neighbour_blocks.shape[2]
    group_size = lax.axis_size("gy")
    pair_count = row_blocks * listed
    capacity = max(2, (pair_count + group_size - 1) // group_size)
    slot_count = group_size * capacity
    query_blocks = queries.reshape(row_blocks, BLOCK, features)
    key_blocks = keys.reshape(row_blocks, BLOCK, features)
    value_blocks = values.reshape(row_blocks, BLOCK, features)
    grad_blocks = out_grad.reshape(row_blocks, BLOCK, features)
    products = out_grad.astype(jnp.float32) * out_attn.astype(jnp.float32)
    delta = products.reshape(row_blocks, BLOCK, HEADS, head_width).sum(-1).astype(jnp.bfloat16)
    delta = delta.transpose(0, 2, 1)
    norm_blocks = log_norm.reshape(HEADS, row_blocks, BLOCK).transpose(1, 0, 2)
    stat_blocks = jnp.stack([norm_blocks, delta], 1)
    row_pack = jnp.stack([query_blocks, grad_blocks], 1)
    key_pack = jnp.stack([key_blocks, value_blocks], 1)
    point_count = tile_x * tile_y * lax.axis_size("gx") * group_size
    columns = neighbour_blocks.reshape(pair_count)
    owners = columns // row_blocks
    inner = columns % row_blocks
    order = jnp.arange(pair_count, dtype=jnp.int32)
    before = (owners[:, None] == owners[None, :]) & (order[None, :] < order[:, None])
    rank = jnp.sum(before.astype(jnp.int32), 1)
    slot_of = owners * capacity + rank
    placed = (jnp.arange(slot_count, dtype=jnp.int32)[:, None] == slot_of[None, :]).astype(
        jnp.float32
    )
    source_rows = (
        (order // listed)[:, None] == jnp.arange(row_blocks, dtype=jnp.int32)[None, :]
    ).astype(jnp.float32)
    picker = jnp.dot(placed, source_rows, precision=lax.Precision.HIGHEST)
    picker_low = picker.astype(jnp.bfloat16)
    send_rows = jnp.dot(
        picker_low, row_pack.reshape(row_blocks, -1), preferred_element_type=jnp.float32
    )
    send_rows = send_rows.astype(jnp.bfloat16).reshape(group_size, capacity, 2, BLOCK, features)
    send_stats = jnp.dot(
        picker_low, stat_blocks.reshape(row_blocks, -1), preferred_element_type=jnp.float32
    )
    send_stats = send_stats.astype(jnp.bfloat16).reshape(group_size, capacity, 2, HEADS, BLOCK)
    send_ids = jnp.dot(placed, (inner + 1).astype(jnp.float32), precision=lax.Precision.HIGHEST)
    send_ids = send_ids.astype(jnp.bfloat16).reshape(group_size, capacity)
    stat_rows = send_stats.reshape(group_size, capacity, 2 * HEADS, BLOCK)
    id_rows = jnp.broadcast_to(send_ids[:, :, None, None], (group_size, capacity, 8, features))
    row_count = 2 * BLOCK
    send_pack = jnp.concatenate(
        [send_rows.reshape(group_size, capacity, row_count, features), stat_rows, id_rows], 2
    )
    slot_rows = send_pack.shape[2]
    edges = jnp.concatenate([out_grad[:, 0], out_grad[:, tile_y - 1]], 0)
    send_pack = jnp.concatenate(
        [
            send_pack.reshape(group_size, capacity * slot_rows, features),
            jnp.broadcast_to(edges[None], (group_size,) + edges.shape),
        ],
        1,
    )
    send_pack, diag_rows, diag_stats, diag_keys = lax.optimization_barrier(
        (send_pack, row_pack, stat_blocks, key_pack)
    )
    pack_in = lax.all_to_all(send_pack, "gy", split_axis=0, concat_axis=0, tiled=True)
    diag_query, diag_key, diag_value = tile_grads(diag_rows, diag_stats, diag_keys)
    pack_in, diag_query, diag_key, diag_value = lax.optimization_barrier(
        (pack_in, diag_query, diag_key, diag_value)
    )
    column = lax.axis_index("gy")
    edge_in = pack_in[:, capacity * slot_rows :]
    before_col = lax.dynamic_index_in_dim(edge_in, (column + group_size - 1) % group_size, 0, False)
    after_col = lax.dynamic_index_in_dim(edge_in, (column + 1) % group_size, 0, False)
    before_col = before_col[tile_x:]
    after_col = after_col[:tile_x]
    grad_x, values_x = lax.optimization_barrier((out_grad, values))
    count_x = lax.axis_size("gx")
    ahead = [(i, (i + 1) % count_x) for i in range(count_x)]
    behind = [((i + 1) % count_x, i) for i in range(count_x)]
    from_before = lax.ppermute(grad_x[tile_x - 1 :], "gx", ahead)
    from_after = lax.ppermute(grad_x[:1], "gx", behind)
    moved = [
        grad_x.astype(jnp.float32),
        jnp.concatenate([grad_x[1:], from_after], 0).astype(jnp.float32),
        jnp.concatenate([from_before, grad_x[:-1]], 0).astype(jnp.float32),
        jnp.concatenate([grad_x[:, 1:], after_col[:, None]], 1).astype(jnp.float32),
        jnp.concatenate([before_col[:, None], grad_x[:, :-1]], 1).astype(jnp.float32),
    ]
    value_float = values_x.astype(jnp.float32)
    stencil_term = stencil[0] * moved[0]
    for index in range(1, 5):
        stencil_term = stencil_term + stencil[index] * moved[index]
    partial_rows = jnp.stack(
        [jnp.sum(moved[index] * value_float, axis=(0, 1)) for index in range(5)]
    )
    point_count = tile_x * tile_y * count_x * group_size
    pack_in = pack_in[:, : capacity * slot_rows].reshape(group_size, capacity, slot_rows, features)
    partial_rows, pack_in = lax.optimization_barrier((partial_rows, pack_in))
    column_sum = gather_sum(partial_rows, "gx")
    rows_in = pack_in[:, :, :row_count].reshape(group_size, capacity, 2, BLOCK, features)
    stats_in = pack_in[:, :, row_count : row_count + 2 * HEADS].reshape(
        group_size, capacity, 2, HEADS, BLOCK
    )
    ids_in = pack_in[:, :, row_count + 2 * HEADS, 0]
    item_count = rows_in.shape[1]
    total_items = group_size * item_count
    wanted = ids_in.astype(jnp.float32).astype(jnp.int32) - 1
    chooser = (wanted[..., None] == jnp.arange(row_blocks, dtype=jnp.int32)).astype(jnp.bfloat16)
    keys_in = jnp.dot(
        chooser.reshape(-1, row_blocks),
        key_pack.reshape(row_blocks, -1),
        preferred_element_type=jnp.float32,
    )
    keys_in = keys_in.astype(jnp.bfloat16).reshape(total_items, 2, BLOCK, features)
    query_part, key_part, value_part = tile_grads(
        rows_in.reshape(total_items, 2, BLOCK, features),
        stats_in.reshape(total_items, 2, HEADS, BLOCK),
        keys_in,
    )
    query_part = query_part.reshape(group_size, item_count, BLOCK, features)
    key_part = key_part.reshape(group_size, item_count, BLOCK, features)
    value_part = value_part.reshape(group_size, item_count, BLOCK, features)
    stencil_count = partial_rows.shape[0]
    stencil_pad = jnp.pad(column_sum, ((0, 8 - stencil_count), (0, 0)))
    return_pack = jnp.concatenate(
        [
            query_part.reshape(group_size, item_count * BLOCK, features),
            jnp.broadcast_to(stencil_pad[None], (group_size, 8, features)),
        ],
        1,
    )
    return_in = lax.all_to_all(return_pack, "gy", split_axis=0, concat_axis=0, tiled=True)
    returned = return_in[:, : item_count * BLOCK]
    summed = jnp.sum(return_in[:, item_count * BLOCK : item_count * BLOCK + stencil_count], 0)
    returned, pieces, ids_in = (returned, jnp.stack([key_part, value_part], 2), ids_in)
    query_sum = diag_query + jnp.einsum(
        "sr,sbf->rbf",
        picker,
        returned.reshape(slot_count, BLOCK, features),
        precision=lax.Precision.HIGHEST,
    )
    arrived = ids_in.reshape(slot_count).astype(jnp.float32).astype(jnp.int32) - 1
    owned = (arrived[:, None] == jnp.arange(row_blocks, dtype=jnp.int32)[None, :]).astype(
        jnp.float32
    )
    key_value_sum = jnp.einsum(
        "sr,sxbf->rxbf",
        owned,
        pieces.reshape(slot_count, 2, BLOCK, features),
        precision=lax.Precision.HIGHEST,
    )
    key_total = diag_key + key_value_sum[:, 0]
    value_total = diag_value + key_value_sum[:, 1]
    stencil_grad = summed / math.sqrt(point_count)
    query_grad = query_sum.reshape(tile_x, tile_y, features).astype(jnp.bfloat16)
    key_grad = key_total.reshape(tile_x, tile_y, features).astype(jnp.bfloat16)
    value_grad = (value_total.reshape(tile_x, tile_y, features) + stencil_term).astype(jnp.bfloat16)
    return (query_grad, key_grad, value_grad, stencil_grad)


def solution(mesh):
    placed = (
        P("gx", "gy", None),
        P("gx", "gy", None),
        P("gx", "gy", None),
        P("gx", "gy", None),
        P("gx", "gy", None),
        P(None, "gx", "gy"),
        P("gx", "gy", None),
        P(),
    )
    return jax.shard_map(
        per_device,
        mesh=mesh,
        in_specs=placed,
        out_specs=(P("gx", "gy", None), P("gx", "gy", None), P("gx", "gy", None), P()),
        check_vma=False,
    )
```

```python
import math

import jax
import jax.numpy as jnp
from jax import lax
from jax.sharding import PartitionSpec as P

BLOCK = 128
HEADS = 4


def with_halo(block, sides, width):
    for axis, dim in sides:
        count = lax.axis_size(axis)
        forward = [(i, i + 1) for i in range(count - 1)]
        forward.append((count - 1, 0))
        backward = [(target, source) for source, target in forward]
        low = lax.ppermute(
            lax.slice_in_dim(block, block.shape[dim] - width, None, axis=dim), axis, forward
        )
        high = lax.ppermute(lax.slice_in_dim(block, 0, width, axis=dim), axis, backward)
        block = jnp.concatenate([low, block, high], axis=dim)
    return block


def prime_factors(count):
    factors = []
    base = 2
    while count > 1:
        while count % base == 0:
            factors.append(base)
            count //= base
        base += 1
    return factors


def exchange_sum(value, axis):
    count = lax.axis_size(axis)
    index = lax.axis_index(axis)
    stride = 1
    for radix in prime_factors(count):
        digit = (index // stride) % radix
        if radix == 2:
            pairs = [(i, i + stride) if (i // stride) % 2 == 0 else (i, i - stride) for i in range(count)]
            value = value + lax.ppermute(value, axis, pairs)
        else:
            received = [value]
            for shift in range(1, radix):
                pairs = []
                for i in range(count):
                    d = (i // stride) % radix
                    pairs.append((i, i + (((d + shift) % radix) - d) * stride))
                received.append(lax.ppermute(value, axis, pairs))
            total = None
            for position in range(radix):
                offset = (digit - position) % radix
                term = received[0]
                for shift in range(1, radix):
                    term = jnp.where(offset == shift, received[shift], term)
                total = term if total is None else total + term
            value = total
        stride *= radix
    return value


def gather_sum(value, axis):
    count = lax.axis_size(axis)
    spread = jnp.broadcast_to(value[None], (count,) + value.shape)
    parts = lax.all_to_all(spread, axis, split_axis=0, concat_axis=0, tiled=True)
    return jnp.sum(parts, axis=0)


def tile_grads(row_pack, stat_pack, key_pack):
    item_count = row_pack.shape[0]
    block_rows = row_pack.shape[2]
    features = row_pack.shape[3]
    head_width = features // HEADS
    softmax_scale = 1.0 / math.sqrt(head_width)
    row_heads = row_pack.reshape(item_count, 2, block_rows, HEADS, head_width).transpose(
        0, 1, 3, 4, 2
    )
    key_heads_all = key_pack.reshape(item_count, 2, block_rows, HEADS, head_width).transpose(
        0, 1, 3, 4, 2
    )
    query_heads = row_heads[:, 0]
    grad_heads = row_heads[:, 1]
    key_heads = key_heads_all[:, 0]
    value_heads = key_heads_all[:, 1]
    log_part = stat_pack[:, 0].astype(jnp.float32)
    delta_part = stat_pack[:, 1].astype(jnp.float32)
    scores = (
        jnp.einsum("shdq,shdk->shqk", query_heads, key_heads, preferred_element_type=jnp.float32)
        * softmax_scale
    )
    weights = jnp.exp(scores - log_part[..., None])
    weight_grad = jnp.einsum(
        "shdq,shdk->shqk", grad_heads, value_heads, preferred_element_type=jnp.float32
    )
    score_grad = weights * (weight_grad - delta_part[..., None])
    weights_low = weights.astype(jnp.bfloat16)
    score_low = score_grad.astype(jnp.bfloat16)
    value_part = jnp.einsum(
        "shqk,shdq->shdk", weights_low, grad_heads, preferred_element_type=jnp.float32
    )
    key_part = (
        jnp.einsum("shqk,shdq->shdk", score_low, query_heads, preferred_element_type=jnp.float32)
        * softmax_scale
    )
    query_part = (
        jnp.einsum("shqk,shdk->shdq", score_low, key_heads, preferred_element_type=jnp.float32)
        * softmax_scale
    )

    def points_last(part):
        return part.reshape(item_count, features, block_rows).transpose(0, 2, 1)

    return (points_last(query_part), points_last(key_part), points_last(value_part))


def per_device(queries, keys, values, out_attn, out_grad, log_norm, neighbour_blocks, stencil):
    tile_x, tile_y, features = queries.shape
    row_blocks = tile_x * tile_y // BLOCK
    head_width = features // HEADS
    listed = neighbour_blocks.shape[2]
    group_size = lax.axis_size("gy")
    pair_count = row_blocks * listed
    capacity = max(2, (pair_count + group_size - 1) // group_size)
    slot_count = group_size * capacity
    query_blocks = queries.reshape(row_blocks, BLOCK, features)
    key_blocks = keys.reshape(row_blocks, BLOCK, features)
    value_blocks = values.reshape(row_blocks, BLOCK, features)
    grad_blocks = out_grad.reshape(row_blocks, BLOCK, features)
    products = out_grad.astype(jnp.float32) * out_attn.astype(jnp.float32)
    delta = products.reshape(row_blocks, BLOCK, HEADS, head_width).sum(-1).astype(jnp.bfloat16)
    delta = delta.transpose(0, 2, 1)
    norm_blocks = log_norm.reshape(HEADS, row_blocks, BLOCK).transpose(1, 0, 2)
    stat_blocks = jnp.stack([norm_blocks, delta], 1)
    row_pack = jnp.stack([query_blocks, grad_blocks], 1)
    key_pack = jnp.stack([key_blocks, value_blocks], 1)
    point_count = tile_x * tile_y * lax.axis_size("gx") * group_size
    columns = neighbour_blocks.reshape(pair_count)
    owners = columns // row_blocks
    inner = columns % row_blocks
    order = jnp.arange(pair_count, dtype=jnp.int32)
    before = (owners[:, None] == owners[None, :]) & (order[None, :] < order[:, None])
    rank = jnp.sum(before.astype(jnp.int32), 1)
    slot_of = owners * capacity + rank
    placed = (jnp.arange(slot_count, dtype=jnp.int32)[:, None] == slot_of[None, :]).astype(
        jnp.float32
    )
    source_rows = (
        (order // listed)[:, None] == jnp.arange(row_blocks, dtype=jnp.int32)[None, :]
    ).astype(jnp.float32)
    picker = jnp.dot(placed, source_rows, precision=lax.Precision.HIGHEST)
    picker_low = picker.astype(jnp.bfloat16)
    send_rows = jnp.dot(
        picker_low, row_pack.reshape(row_blocks, -1), preferred_element_type=jnp.float32
    )
    send_rows = send_rows.astype(jnp.bfloat16).reshape(group_size, capacity, 2, BLOCK, features)
    send_stats = jnp.dot(
        picker_low, stat_blocks.reshape(row_blocks, -1), preferred_element_type=jnp.float32
    )
    send_stats = send_stats.astype(jnp.bfloat16).reshape(group_size, capacity, 2, HEADS, BLOCK)
    send_ids = jnp.dot(placed, (inner + 1).astype(jnp.float32), precision=lax.Precision.HIGHEST)
    send_ids = send_ids.astype(jnp.bfloat16).reshape(group_size, capacity)
    stat_rows = send_stats.reshape(group_size, capacity, 2 * HEADS, BLOCK)
    id_rows = jnp.broadcast_to(send_ids[:, :, None, None], (group_size, capacity, 8, features))
    row_count = 2 * BLOCK
    send_pack = jnp.concatenate(
        [send_rows.reshape(group_size, capacity, row_count, features), stat_rows, id_rows], 2
    )
    slot_rows = send_pack.shape[2]
    edges = jnp.concatenate([out_grad[:, 0], out_grad[:, tile_y - 1]], 0)
    send_pack = jnp.concatenate(
        [
            send_pack.reshape(group_size, capacity * slot_rows, features),
            jnp.broadcast_to(edges[None], (group_size,) + edges.shape),
        ],
        1,
    )
    send_pack, diag_rows, diag_stats, diag_keys = lax.optimization_barrier(
        (send_pack, row_pack, stat_blocks, key_pack)
    )
    pack_in = lax.all_to_all(send_pack, "gy", split_axis=0, concat_axis=0, tiled=True)
    diag_query, diag_key, diag_value = tile_grads(diag_rows, diag_stats, diag_keys)
    pack_in, diag_query, diag_key, diag_value = lax.optimization_barrier(
        (pack_in, diag_query, diag_key, diag_value)
    )
    column = lax.axis_index("gy")
    edge_in = pack_in[:, capacity * slot_rows :]
    before_col = lax.dynamic_index_in_dim(edge_in, (column + group_size - 1) % group_size, 0, False)
    after_col = lax.dynamic_index_in_dim(edge_in, (column + 1) % group_size, 0, False)
    before_col = before_col[tile_x:]
    after_col = after_col[:tile_x]
    grad_x, values_x = lax.optimization_barrier((out_grad, values))
    count_x = lax.axis_size("gx")
    ahead = [(i, (i + 1) % count_x) for i in range(count_x)]
    behind = [((i + 1) % count_x, i) for i in range(count_x)]
    from_before = lax.ppermute(grad_x[tile_x - 1 :], "gx", ahead)
    from_after = lax.ppermute(grad_x[:1], "gx", behind)
    moved = [
        grad_x.astype(jnp.float32),
        jnp.concatenate([grad_x[1:], from_after], 0).astype(jnp.float32),
        jnp.concatenate([from_before, grad_x[:-1]], 0).astype(jnp.float32),
        jnp.concatenate([grad_x[:, 1:], after_col[:, None]], 1).astype(jnp.float32),
        jnp.concatenate([before_col[:, None], grad_x[:, :-1]], 1).astype(jnp.float32),
    ]
    value_float = values_x.astype(jnp.float32)
    stencil_term = stencil[0] * moved[0]
    for index in range(1, 5):
        stencil_term = stencil_term + stencil[index] * moved[index]
    partial_rows = jnp.stack(
        [jnp.sum(moved[index] * value_float, axis=(0, 1)) for index in range(5)]
    )
    point_count = tile_x * tile_y * count_x * group_size
    pack_in = pack_in[:, : capacity * slot_rows].reshape(group_size, capacity, slot_rows, features)
    partial_rows, pack_in = lax.optimization_barrier((partial_rows, pack_in))
    column_sum = gather_sum(partial_rows, "gx")
    rows_in = pack_in[:, :, :row_count].reshape(group_size, capacity, 2, BLOCK, features)
    stats_in = pack_in[:, :, row_count : row_count + 2 * HEADS].reshape(
        group_size, capacity, 2, HEADS, BLOCK
    )
    ids_in = pack_in[:, :, row_count + 2 * HEADS, 0]
    item_count = rows_in.shape[1]
    total_items = group_size * item_count
    wanted = ids_in.astype(jnp.float32).astype(jnp.int32) - 1
    chooser = (wanted[..., None] == jnp.arange(row_blocks, dtype=jnp.int32)).astype(jnp.bfloat16)
    keys_in = jnp.dot(
        chooser.reshape(-1, row_blocks),
        key_pack.reshape(row_blocks, -1),
        preferred_element_type=jnp.float32,
    )
    keys_in = keys_in.astype(jnp.bfloat16).reshape(total_items, 2, BLOCK, features)
    query_part, key_part, value_part = tile_grads(
        rows_in.reshape(total_items, 2, BLOCK, features),
        stats_in.reshape(total_items, 2, HEADS, BLOCK),
        keys_in,
    )
    query_part = query_part.reshape(group_size, item_count, BLOCK, features)
    key_part = key_part.reshape(group_size, item_count, BLOCK, features)
    value_part = value_part.reshape(group_size, item_count, BLOCK, features)
    stencil_count = partial_rows.shape[0]
    stencil_hi = column_sum.astype(jnp.bfloat16)
    stencil_rest = column_sum - stencil_hi.astype(jnp.float32)
    stencil_mid = stencil_rest.astype(jnp.bfloat16)
    stencil_lo = (stencil_rest - stencil_mid.astype(jnp.float32)).astype(jnp.bfloat16)
    stencil_terms = jnp.concatenate([stencil_hi, stencil_mid, stencil_lo], 0)
    term_rows = 3 * stencil_count
    stencil_pad = jnp.pad(stencil_terms, ((0, 16 - term_rows), (0, 0)))
    return_pack = jnp.concatenate(
        [
            query_part.reshape(group_size, item_count * BLOCK, features).astype(jnp.bfloat16),
            jnp.broadcast_to(stencil_pad[None], (group_size, 16, features)),
        ],
        1,
    )
    return_in = lax.all_to_all(return_pack, "gy", split_axis=0, concat_axis=0, tiled=True)
    returned = return_in[:, : item_count * BLOCK].astype(jnp.float32)
    terms_in = return_in[:, item_count * BLOCK : item_count * BLOCK + term_rows].astype(jnp.float32)
    terms_in = terms_in.reshape(group_size, 3, stencil_count, features)
    summed = jnp.sum(terms_in[:, 0] + terms_in[:, 1] + terms_in[:, 2], 0)
    returned, pieces, ids_in = (returned, jnp.stack([key_part, value_part], 2), ids_in)
    query_sum = diag_query + jnp.einsum(
        "sr,sbf->rbf",
        picker,
        returned.reshape(slot_count, BLOCK, features),
        precision=lax.Precision.HIGHEST,
    )
    arrived = ids_in.reshape(slot_count).astype(jnp.float32).astype(jnp.int32) - 1
    owned = (arrived[:, None] == jnp.arange(row_blocks, dtype=jnp.int32)[None, :]).astype(
        jnp.float32
    )
    key_value_sum = jnp.einsum(
        "sr,sxbf->rxbf",
        owned,
        pieces.reshape(slot_count, 2, BLOCK, features),
        precision=lax.Precision.HIGHEST,
    )
    key_total = diag_key + key_value_sum[:, 0]
    value_total = diag_value + key_value_sum[:, 1]
    stencil_grad = summed / math.sqrt(point_count)
    query_grad = query_sum.reshape(tile_x, tile_y, features).astype(jnp.bfloat16)
    key_grad = key_total.reshape(tile_x, tile_y, features).astype(jnp.bfloat16)
    value_grad = (value_total.reshape(tile_x, tile_y, features) + stencil_term).astype(jnp.bfloat16)
    return (query_grad, key_grad, value_grad, stencil_grad)


def solution(mesh):
    placed = (
        P("gx", "gy", None),
        P("gx", "gy", None),
        P("gx", "gy", None),
        P("gx", "gy", None),
        P("gx", "gy", None),
        P(None, "gx", "gy"),
        P("gx", "gy", None),
        P(),
    )
    return jax.shard_map(
        per_device,
        mesh=mesh,
        in_specs=placed,
        out_specs=(P("gx", "gy", None), P("gx", "gy", None), P("gx", "gy", None), P()),
        check_vma=False,
    )
```

```python
import math

import jax
import jax.numpy as jnp
from jax import lax
from jax.sharding import PartitionSpec as P

BLOCK = 128
HEADS = 4


def with_halo(block, sides, width):
    for axis, dim in sides:
        count = lax.axis_size(axis)
        forward = [(i, i + 1) for i in range(count - 1)]
        forward.append((count - 1, 0))
        backward = [(target, source) for source, target in forward]
        low = lax.ppermute(
            lax.slice_in_dim(block, block.shape[dim] - width, None, axis=dim), axis, forward
        )
        high = lax.ppermute(lax.slice_in_dim(block, 0, width, axis=dim), axis, backward)
        block = jnp.concatenate([low, block, high], axis=dim)
    return block


def prime_factors(count):
    factors = []
    base = 2
    while count > 1:
        while count % base == 0:
            factors.append(base)
            count //= base
        base += 1
    return factors


def exchange_sum(value, axis):
    count = lax.axis_size(axis)
    index = lax.axis_index(axis)
    stride = 1
    for radix in prime_factors(count):
        digit = (index // stride) % radix
        if radix == 2:
            pairs = [(i, i + stride) if (i // stride) % 2 == 0 else (i, i - stride) for i in range(count)]
            value = value + lax.ppermute(value, axis, pairs)
        else:
            received = [value]
            for shift in range(1, radix):
                pairs = []
                for i in range(count):
                    d = (i // stride) % radix
                    pairs.append((i, i + (((d + shift) % radix) - d) * stride))
                received.append(lax.ppermute(value, axis, pairs))
            total = None
            for position in range(radix):
                offset = (digit - position) % radix
                term = received[0]
                for shift in range(1, radix):
                    term = jnp.where(offset == shift, received[shift], term)
                total = term if total is None else total + term
            value = total
        stride *= radix
    return value


def gather_sum(value, axis):
    count = lax.axis_size(axis)
    spread = jnp.broadcast_to(value[None], (count,) + value.shape)
    parts = lax.all_to_all(spread, axis, split_axis=0, concat_axis=0, tiled=True)
    return jnp.sum(parts, axis=0)


def tile_grads(row_pack, stat_pack, key_pack):
    features = row_pack.shape[3]
    head_width = features // HEADS
    softmax_scale = 1.0 / math.sqrt(head_width)
    head_of = jnp.arange(features, dtype=jnp.int32) // head_width
    mask = (head_of[None, :] == jnp.arange(HEADS, dtype=jnp.int32)[:, None]).astype(row_pack.dtype)

    def spread(part):
        return part[:, None] * mask[None, :, None, :]

    query_rows = row_pack[:, 0]
    grad_rows = row_pack[:, 1]
    key_rows = key_pack[:, 0]
    value_rows = key_pack[:, 1]
    query_heads = spread(query_rows)
    grad_heads = spread(grad_rows)
    key_heads = spread(key_rows)
    log_part = stat_pack[:, 0].astype(jnp.float32)
    delta_part = stat_pack[:, 1].astype(jnp.float32)
    scores = (
        jnp.einsum("shqf,skf->shqk", query_heads, key_rows, preferred_element_type=jnp.float32)
        * softmax_scale
    )
    weights = jnp.exp(scores - log_part[..., None])
    weight_grad = jnp.einsum(
        "shqf,skf->shqk", grad_heads, value_rows, preferred_element_type=jnp.float32
    )
    score_grad = weights * (weight_grad - delta_part[..., None])
    weights_low = weights.astype(jnp.bfloat16)
    score_low = score_grad.astype(jnp.bfloat16)
    value_part = jnp.einsum(
        "shqk,shqf->skf", weights_low, grad_heads, preferred_element_type=jnp.float32
    )
    key_part = (
        jnp.einsum("shqk,shqf->skf", score_low, query_heads, preferred_element_type=jnp.float32)
        * softmax_scale
    )
    query_part = (
        jnp.einsum("shqk,shkf->sqf", score_low, key_heads, preferred_element_type=jnp.float32)
        * softmax_scale
    )
    return (query_part, key_part, value_part)


def per_device(queries, keys, values, out_attn, out_grad, log_norm, neighbour_blocks, stencil):
    tile_x, tile_y, features = queries.shape
    row_blocks = tile_x * tile_y // BLOCK
    head_width = features // HEADS
    listed = neighbour_blocks.shape[2]
    group_size = lax.axis_size("gy")
    pair_count = row_blocks * listed
    capacity = max(2, (pair_count + group_size - 1) // group_size)
    slot_count = group_size * capacity
    query_blocks = queries.reshape(row_blocks, BLOCK, features)
    key_blocks = keys.reshape(row_blocks, BLOCK, features)
    value_blocks = values.reshape(row_blocks, BLOCK, features)
    grad_blocks = out_grad.reshape(row_blocks, BLOCK, features)
    products = out_grad.astype(jnp.float32) * out_attn.astype(jnp.float32)
    delta = products.reshape(row_blocks, BLOCK, HEADS, head_width).sum(-1).astype(jnp.bfloat16)
    delta = delta.transpose(0, 2, 1)
    norm_blocks = log_norm.reshape(HEADS, row_blocks, BLOCK).transpose(1, 0, 2)
    stat_blocks = jnp.stack([norm_blocks, delta], 1)
    row_pack = jnp.stack([query_blocks, grad_blocks], 1)
    key_pack = jnp.stack([key_blocks, value_blocks], 1)
    point_count = tile_x * tile_y * lax.axis_size("gx") * group_size
    columns = neighbour_blocks.reshape(pair_count)
    owners = columns // row_blocks
    inner = columns % row_blocks
    order = jnp.arange(pair_count, dtype=jnp.int32)
    before = (owners[:, None] == owners[None, :]) & (order[None, :] < order[:, None])
    rank = jnp.sum(before.astype(jnp.int32), 1)
    slot_of = owners * capacity + rank
    placed = (jnp.arange(slot_count, dtype=jnp.int32)[:, None] == slot_of[None, :]).astype(
        jnp.float32
    )
    source_rows = (
        (order // listed)[:, None] == jnp.arange(row_blocks, dtype=jnp.int32)[None, :]
    ).astype(jnp.float32)
    picker = jnp.dot(placed, source_rows, precision=lax.Precision.HIGHEST)
    picker_low = picker.astype(jnp.bfloat16)
    send_rows = jnp.dot(
        picker_low, row_pack.reshape(row_blocks, -1), preferred_element_type=jnp.float32
    )
    send_rows = send_rows.astype(jnp.bfloat16).reshape(group_size, capacity, 2, BLOCK, features)
    send_stats = jnp.dot(
        picker_low, stat_blocks.reshape(row_blocks, -1), preferred_element_type=jnp.float32
    )
    send_stats = send_stats.astype(jnp.bfloat16).reshape(group_size, capacity, 2, HEADS, BLOCK)
    send_ids = jnp.dot(placed, (inner + 1).astype(jnp.float32), precision=lax.Precision.HIGHEST)
    send_ids = send_ids.astype(jnp.bfloat16).reshape(group_size, capacity)
    stat_rows = send_stats.reshape(group_size, capacity, 2 * HEADS, BLOCK)
    id_rows = jnp.broadcast_to(send_ids[:, :, None, None], (group_size, capacity, 8, features))
    row_count = 2 * BLOCK
    send_pack = jnp.concatenate(
        [send_rows.reshape(group_size, capacity, row_count, features), stat_rows, id_rows], 2
    )
    slot_rows = send_pack.shape[2]
    edges = jnp.concatenate([out_grad[:, 0], out_grad[:, tile_y - 1]], 0)
    send_pack = jnp.concatenate(
        [
            send_pack.reshape(group_size, capacity * slot_rows, features),
            jnp.broadcast_to(edges[None], (group_size,) + edges.shape),
        ],
        1,
    )
    send_pack, diag_rows, diag_stats, diag_keys = lax.optimization_barrier(
        (send_pack, row_pack, stat_blocks, key_pack)
    )
    pack_in = lax.all_to_all(send_pack, "gy", split_axis=0, concat_axis=0, tiled=True)
    diag_query, diag_key, diag_value = tile_grads(diag_rows, diag_stats, diag_keys)
    pack_in, diag_query, diag_key, diag_value = lax.optimization_barrier(
        (pack_in, diag_query, diag_key, diag_value)
    )
    column = lax.axis_index("gy")
    edge_in = pack_in[:, capacity * slot_rows :]
    before_col = lax.dynamic_index_in_dim(edge_in, (column + group_size - 1) % group_size, 0, False)
    after_col = lax.dynamic_index_in_dim(edge_in, (column + 1) % group_size, 0, False)
    before_col = before_col[tile_x:]
    after_col = after_col[:tile_x]
    grad_x, values_x = lax.optimization_barrier((out_grad, values))
    count_x = lax.axis_size("gx")
    ahead = [(i, (i + 1) % count_x) for i in range(count_x)]
    behind = [((i + 1) % count_x, i) for i in range(count_x)]
    from_before = lax.ppermute(grad_x[tile_x - 1 :], "gx", ahead)
    from_after = lax.ppermute(grad_x[:1], "gx", behind)
    moved = [
        grad_x.astype(jnp.float32),
        jnp.concatenate([grad_x[1:], from_after], 0).astype(jnp.float32),
        jnp.concatenate([from_before, grad_x[:-1]], 0).astype(jnp.float32),
        jnp.concatenate([grad_x[:, 1:], after_col[:, None]], 1).astype(jnp.float32),
        jnp.concatenate([before_col[:, None], grad_x[:, :-1]], 1).astype(jnp.float32),
    ]
    value_float = values_x.astype(jnp.float32)
    stencil_term = stencil[0] * moved[0]
    for index in range(1, 5):
        stencil_term = stencil_term + stencil[index] * moved[index]
    partial_rows = jnp.stack(
        [jnp.sum(moved[index] * value_float, axis=(0, 1)) for index in range(5)]
    )
    point_count = tile_x * tile_y * count_x * group_size
    pack_in = pack_in[:, : capacity * slot_rows].reshape(group_size, capacity, slot_rows, features)
    partial_rows, pack_in = lax.optimization_barrier((partial_rows, pack_in))
    column_sum = gather_sum(partial_rows, "gx")
    rows_in = pack_in[:, :, :row_count].reshape(group_size, capacity, 2, BLOCK, features)
    stats_in = pack_in[:, :, row_count : row_count + 2 * HEADS].reshape(
        group_size, capacity, 2, HEADS, BLOCK
    )
    ids_in = pack_in[:, :, row_count + 2 * HEADS, 0]
    item_count = rows_in.shape[1]
    total_items = group_size * item_count
    wanted = ids_in.astype(jnp.float32).astype(jnp.int32) - 1
    chooser = (wanted[..., None] == jnp.arange(row_blocks, dtype=jnp.int32)).astype(jnp.bfloat16)
    keys_in = jnp.dot(
        chooser.reshape(-1, row_blocks),
        key_pack.reshape(row_blocks, -1),
        preferred_element_type=jnp.float32,
    )
    keys_in = keys_in.astype(jnp.bfloat16).reshape(total_items, 2, BLOCK, features)
    query_part, key_part, value_part = tile_grads(
        rows_in.reshape(total_items, 2, BLOCK, features),
        stats_in.reshape(total_items, 2, HEADS, BLOCK),
        keys_in,
    )
    query_part = query_part.reshape(group_size, item_count, BLOCK, features)
    key_part = key_part.reshape(group_size, item_count, BLOCK, features)
    value_part = value_part.reshape(group_size, item_count, BLOCK, features)
    stencil_count = partial_rows.shape[0]
    stencil_hi = column_sum.astype(jnp.bfloat16)
    stencil_rest = column_sum - stencil_hi.astype(jnp.float32)
    stencil_mid = stencil_rest.astype(jnp.bfloat16)
    stencil_lo = (stencil_rest - stencil_mid.astype(jnp.float32)).astype(jnp.bfloat16)
    stencil_terms = jnp.concatenate([stencil_hi, stencil_mid, stencil_lo], 0)
    term_rows = 3 * stencil_count
    stencil_pad = jnp.pad(stencil_terms, ((0, 16 - term_rows), (0, 0)))
    return_pack = jnp.concatenate(
        [
            query_part.reshape(group_size, item_count * BLOCK, features).astype(jnp.bfloat16),
            jnp.broadcast_to(stencil_pad[None], (group_size, 16, features)),
        ],
        1,
    )
    return_in = lax.all_to_all(return_pack, "gy", split_axis=0, concat_axis=0, tiled=True)
    returned = return_in[:, : item_count * BLOCK].astype(jnp.float32)
    terms_in = return_in[:, item_count * BLOCK : item_count * BLOCK + term_rows].astype(jnp.float32)
    terms_in = terms_in.reshape(group_size, 3, stencil_count, features)
    summed = jnp.sum(terms_in[:, 0] + terms_in[:, 1] + terms_in[:, 2], 0)
    returned, pieces, ids_in = (returned, jnp.stack([key_part, value_part], 2), ids_in)
    query_sum = diag_query + jnp.einsum(
        "sr,sbf->rbf",
        picker,
        returned.reshape(slot_count, BLOCK, features),
        precision=lax.Precision.HIGHEST,
    )
    arrived = ids_in.reshape(slot_count).astype(jnp.float32).astype(jnp.int32) - 1
    owned = (arrived[:, None] == jnp.arange(row_blocks, dtype=jnp.int32)[None, :]).astype(
        jnp.float32
    )
    key_value_sum = jnp.einsum(
        "sr,sxbf->rxbf",
        owned,
        pieces.reshape(slot_count, 2, BLOCK, features),
        precision=lax.Precision.HIGHEST,
    )
    key_total = diag_key + key_value_sum[:, 0]
    value_total = diag_value + key_value_sum[:, 1]
    stencil_grad = summed / math.sqrt(point_count)
    query_grad = query_sum.reshape(tile_x, tile_y, features).astype(jnp.bfloat16)
    key_grad = key_total.reshape(tile_x, tile_y, features).astype(jnp.bfloat16)
    value_grad = (value_total.reshape(tile_x, tile_y, features) + stencil_term).astype(jnp.bfloat16)
    return (query_grad, key_grad, value_grad, stencil_grad)


def solution(mesh):
    placed = (
        P("gx", "gy", None),
        P("gx", "gy", None),
        P("gx", "gy", None),
        P("gx", "gy", None),
        P("gx", "gy", None),
        P(None, "gx", "gy"),
        P("gx", "gy", None),
        P(),
    )
    return jax.shard_map(
        per_device,
        mesh=mesh,
        in_specs=placed,
        out_specs=(P("gx", "gy", None), P("gx", "gy", None), P("gx", "gy", None), P()),
        check_vma=False,
    )
```

```python
import math

import jax
import jax.numpy as jnp
from jax import lax
from jax.sharding import PartitionSpec as P

BLOCK = 128
HEADS = 4
OUTER = "gx_outer"
INNER = "gx_inner"
PLANE = 8


def prime_factors(count):
    factors = []
    base = 2
    while count > 1:
        while count % base == 0:
            factors.append(base)
            count //= base
        base += 1
    return factors


def exchange_sum(value, axis):
    count = lax.axis_size(axis)
    index = lax.axis_index(axis)
    stride = 1
    for radix in prime_factors(count):
        digit = (index // stride) % radix
        if radix == 2:
            pairs = [(i, i + stride) if (i // stride) % 2 == 0 else (i, i - stride) for i in range(count)]
            value = value + lax.ppermute(value, axis, pairs)
        else:
            received = [value]
            for shift in range(1, radix):
                pairs = []
                for i in range(count):
                    d = (i // stride) % radix
                    pairs.append((i, i + (((d + shift) % radix) - d) * stride))
                received.append(lax.ppermute(value, axis, pairs))
            total = None
            for position in range(radix):
                offset = (digit - position) % radix
                term = received[0]
                for shift in range(1, radix):
                    term = jnp.where(offset == shift, received[shift], term)
                total = term if total is None else total + term
            value = total
        stride *= radix
    return value


def gather_sum(value, axis):
    count = lax.axis_size(axis)
    spread = jnp.broadcast_to(value[None], (count,) + value.shape)
    parts = lax.all_to_all(spread, axis, split_axis=0, concat_axis=0, tiled=True)
    return jnp.sum(parts, axis=0)


def tile_grads(row_pack, stat_pack, key_pack):
    features = row_pack.shape[3]
    head_width = features // HEADS
    softmax_scale = 1.0 / math.sqrt(head_width)
    head_of = jnp.arange(features, dtype=jnp.int32) // head_width
    mask = (head_of[None, :] == jnp.arange(HEADS, dtype=jnp.int32)[:, None]).astype(row_pack.dtype)

    def spread(part):
        return part[:, None] * mask[None, :, None, :]

    query_rows = row_pack[:, 0]
    grad_rows = row_pack[:, 1]
    key_rows = key_pack[:, 0]
    value_rows = key_pack[:, 1]
    query_heads = spread(query_rows)
    grad_heads = spread(grad_rows)
    key_heads = spread(key_rows)
    log_part = stat_pack[:, 0].astype(jnp.float32)
    delta_part = stat_pack[:, 1].astype(jnp.float32)
    scores = (
        jnp.einsum("shqf,skf->shqk", query_heads, key_rows, preferred_element_type=jnp.float32)
        * softmax_scale
    )
    weights = jnp.exp(scores - log_part[..., None])
    weight_grad = jnp.einsum(
        "shqf,skf->shqk", grad_heads, value_rows, preferred_element_type=jnp.float32
    )
    score_grad = weights * (weight_grad - delta_part[..., None])
    weights_low = weights.astype(jnp.bfloat16)
    score_low = score_grad.astype(jnp.bfloat16)
    value_part = jnp.einsum(
        "shqk,shqf->skf", weights_low, grad_heads, preferred_element_type=jnp.float32
    )
    key_part = (
        jnp.einsum("shqk,shqf->skf", score_low, query_heads, preferred_element_type=jnp.float32)
        * softmax_scale
    )
    query_part = (
        jnp.einsum("shqk,shkf->sqf", score_low, key_heads, preferred_element_type=jnp.float32)
        * softmax_scale
    )
    return (query_part, key_part, value_part)


def per_device(queries, keys, values, out_attn, out_grad, log_norm, neighbour_blocks, stencil):
    tile_x, tile_y, features = queries.shape
    row_blocks = tile_x * tile_y // BLOCK
    head_width = features // HEADS
    listed = neighbour_blocks.shape[2]
    group_size = lax.axis_size("gy")
    pair_count = row_blocks * listed
    capacity = max(2, (pair_count + group_size - 1) // group_size)
    slot_count = group_size * capacity
    query_blocks = queries.reshape(row_blocks, BLOCK, features)
    key_blocks = keys.reshape(row_blocks, BLOCK, features)
    value_blocks = values.reshape(row_blocks, BLOCK, features)
    grad_blocks = out_grad.reshape(row_blocks, BLOCK, features)
    products = out_grad.astype(jnp.float32) * out_attn.astype(jnp.float32)
    delta = products.reshape(row_blocks, BLOCK, HEADS, head_width).sum(-1).astype(jnp.bfloat16)
    delta = delta.transpose(0, 2, 1)
    norm_blocks = log_norm.reshape(HEADS, row_blocks, BLOCK).transpose(1, 0, 2)
    stat_blocks = jnp.stack([norm_blocks, delta], 1)
    row_pack = jnp.stack([query_blocks, grad_blocks], 1)
    key_pack = jnp.stack([key_blocks, value_blocks], 1)
    point_count = tile_x * tile_y * (lax.axis_size(OUTER) * lax.axis_size(INNER)) * group_size
    columns = neighbour_blocks.reshape(pair_count)
    owners = columns // row_blocks
    inner = columns % row_blocks
    order = jnp.arange(pair_count, dtype=jnp.int32)
    before = (owners[:, None] == owners[None, :]) & (order[None, :] < order[:, None])
    rank = jnp.sum(before.astype(jnp.int32), 1)
    slot_of = owners * capacity + rank
    placed = (jnp.arange(slot_count, dtype=jnp.int32)[:, None] == slot_of[None, :]).astype(
        jnp.float32
    )
    source_rows = (
        (order // listed)[:, None] == jnp.arange(row_blocks, dtype=jnp.int32)[None, :]
    ).astype(jnp.float32)
    picker = jnp.dot(placed, source_rows, precision=lax.Precision.HIGHEST)
    picker_low = picker.astype(jnp.bfloat16)
    send_rows = jnp.dot(
        picker_low, row_pack.reshape(row_blocks, -1), preferred_element_type=jnp.float32
    )
    send_rows = send_rows.astype(jnp.bfloat16).reshape(group_size, capacity, 2, BLOCK, features)
    send_stats = jnp.dot(
        picker_low, stat_blocks.reshape(row_blocks, -1), preferred_element_type=jnp.float32
    )
    send_stats = send_stats.astype(jnp.bfloat16).reshape(group_size, capacity, 2, HEADS, BLOCK)
    send_ids = jnp.dot(placed, (inner + 1).astype(jnp.float32), precision=lax.Precision.HIGHEST)
    send_ids = send_ids.astype(jnp.bfloat16).reshape(group_size, capacity)
    stat_rows = send_stats.reshape(group_size, capacity, 2 * HEADS, BLOCK)
    id_rows = jnp.broadcast_to(send_ids[:, :, None, None], (group_size, capacity, 8, features))
    row_count = 2 * BLOCK
    send_pack = jnp.concatenate(
        [send_rows.reshape(group_size, capacity, row_count, features), stat_rows, id_rows], 2
    )
    slot_rows = send_pack.shape[2]
    edges = jnp.concatenate([out_grad[:, 0], out_grad[:, tile_y - 1]], 0)
    send_pack = jnp.concatenate(
        [
            send_pack.reshape(group_size, capacity * slot_rows, features),
            jnp.broadcast_to(edges[None], (group_size,) + edges.shape),
        ],
        1,
    )
    send_pack, diag_rows, diag_stats, diag_keys = lax.optimization_barrier(
        (send_pack, row_pack, stat_blocks, key_pack)
    )
    pack_in = lax.all_to_all(send_pack, "gy", split_axis=0, concat_axis=0, tiled=True)
    diag_query, diag_key, diag_value = tile_grads(diag_rows, diag_stats, diag_keys)
    pack_in, diag_query, diag_key, diag_value = lax.optimization_barrier(
        (pack_in, diag_query, diag_key, diag_value)
    )
    column = lax.axis_index("gy")
    edge_in = pack_in[:, capacity * slot_rows :]
    before_col = lax.dynamic_index_in_dim(edge_in, (column + group_size - 1) % group_size, 0, False)
    after_col = lax.dynamic_index_in_dim(edge_in, (column + 1) % group_size, 0, False)
    before_col = before_col[tile_x:]
    after_col = after_col[:tile_x]
    grad_x, values_x = lax.optimization_barrier((out_grad, values))
    count_x = (lax.axis_size(OUTER) * lax.axis_size(INNER))
    ahead = [(i, (i + 1) % count_x) for i in range(count_x)]
    behind = [((i + 1) % count_x, i) for i in range(count_x)]
    from_before = lax.ppermute(grad_x[tile_x - 1 :], (OUTER, INNER), ahead)
    from_after = lax.ppermute(grad_x[:1], (OUTER, INNER), behind)
    moved = [
        grad_x.astype(jnp.float32),
        jnp.concatenate([grad_x[1:], from_after], 0).astype(jnp.float32),
        jnp.concatenate([from_before, grad_x[:-1]], 0).astype(jnp.float32),
        jnp.concatenate([grad_x[:, 1:], after_col[:, None]], 1).astype(jnp.float32),
        jnp.concatenate([before_col[:, None], grad_x[:, :-1]], 1).astype(jnp.float32),
    ]
    value_float = values_x.astype(jnp.float32)
    stencil_term = stencil[0] * moved[0]
    for index in range(1, 5):
        stencil_term = stencil_term + stencil[index] * moved[index]
    partial_rows = jnp.stack(
        [jnp.sum(moved[index] * value_float, axis=(0, 1)) for index in range(5)]
    )
    point_count = tile_x * tile_y * count_x * group_size
    pack_in = pack_in[:, : capacity * slot_rows].reshape(group_size, capacity, slot_rows, features)
    partial_rows, pack_in = lax.optimization_barrier((partial_rows, pack_in))
    column_sum = gather_sum(gather_sum(partial_rows, INNER), OUTER)
    rows_in = pack_in[:, :, :row_count].reshape(group_size, capacity, 2, BLOCK, features)
    stats_in = pack_in[:, :, row_count : row_count + 2 * HEADS].reshape(
        group_size, capacity, 2, HEADS, BLOCK
    )
    ids_in = pack_in[:, :, row_count + 2 * HEADS, 0]
    item_count = rows_in.shape[1]
    total_items = group_size * item_count
    wanted = ids_in.astype(jnp.float32).astype(jnp.int32) - 1
    chooser = (wanted[..., None] == jnp.arange(row_blocks, dtype=jnp.int32)).astype(jnp.bfloat16)
    keys_in = jnp.dot(
        chooser.reshape(-1, row_blocks),
        key_pack.reshape(row_blocks, -1),
        preferred_element_type=jnp.float32,
    )
    keys_in = keys_in.astype(jnp.bfloat16).reshape(total_items, 2, BLOCK, features)
    query_part, key_part, value_part = tile_grads(
        rows_in.reshape(total_items, 2, BLOCK, features),
        stats_in.reshape(total_items, 2, HEADS, BLOCK),
        keys_in,
    )
    query_part = query_part.reshape(group_size, item_count, BLOCK, features)
    key_part = key_part.reshape(group_size, item_count, BLOCK, features)
    value_part = value_part.reshape(group_size, item_count, BLOCK, features)
    stencil_count = partial_rows.shape[0]
    stencil_hi = column_sum.astype(jnp.bfloat16)
    stencil_rest = column_sum - stencil_hi.astype(jnp.float32)
    stencil_mid = stencil_rest.astype(jnp.bfloat16)
    stencil_lo = (stencil_rest - stencil_mid.astype(jnp.float32)).astype(jnp.bfloat16)
    stencil_terms = jnp.concatenate([stencil_hi, stencil_mid, stencil_lo], 0)
    term_rows = 3 * stencil_count
    stencil_pad = jnp.pad(stencil_terms, ((0, 16 - term_rows), (0, 0)))
    return_pack = jnp.concatenate(
        [
            query_part.reshape(group_size, item_count * BLOCK, features).astype(jnp.bfloat16),
            jnp.broadcast_to(stencil_pad[None], (group_size, 16, features)),
        ],
        1,
    )
    return_in = lax.all_to_all(return_pack, "gy", split_axis=0, concat_axis=0, tiled=True)
    returned = return_in[:, : item_count * BLOCK].astype(jnp.float32)
    terms_in = return_in[:, item_count * BLOCK : item_count * BLOCK + term_rows].astype(jnp.float32)
    terms_in = terms_in.reshape(group_size, 3, stencil_count, features)
    summed = jnp.sum(terms_in[:, 0] + terms_in[:, 1] + terms_in[:, 2], 0)
    returned, pieces, ids_in = (returned, jnp.stack([key_part, value_part], 2), ids_in)
    query_sum = diag_query + jnp.einsum(
        "sr,sbf->rbf",
        picker,
        returned.reshape(slot_count, BLOCK, features),
        precision=lax.Precision.HIGHEST,
    )
    arrived = ids_in.reshape(slot_count).astype(jnp.float32).astype(jnp.int32) - 1
    owned = (arrived[:, None] == jnp.arange(row_blocks, dtype=jnp.int32)[None, :]).astype(
        jnp.float32
    )
    key_value_sum = jnp.einsum(
        "sr,sxbf->rxbf",
        owned,
        pieces.reshape(slot_count, 2, BLOCK, features),
        precision=lax.Precision.HIGHEST,
    )
    key_total = diag_key + key_value_sum[:, 0]
    value_total = diag_value + key_value_sum[:, 1]
    stencil_grad = summed / math.sqrt(point_count)
    query_grad = query_sum.reshape(tile_x, tile_y, features).astype(jnp.bfloat16)
    key_grad = key_total.reshape(tile_x, tile_y, features).astype(jnp.bfloat16)
    value_grad = (value_total.reshape(tile_x, tile_y, features) + stencil_term).astype(jnp.bfloat16)
    return (query_grad, key_grad, value_grad, stencil_grad)


def solution(mesh):
    rows = mesh.shape["gx"]
    inner = PLANE if rows % PLANE == 0 else 1
    fine = jax.sharding.Mesh(
        mesh.devices.reshape(rows // inner, inner, mesh.shape["gy"]), (OUTER, INNER, "gy")
    )
    split = (OUTER, INNER)
    placed = (
        P(split, "gy", None),
        P(split, "gy", None),
        P(split, "gy", None),
        P(split, "gy", None),
        P(split, "gy", None),
        P(None, split, "gy"),
        P(split, "gy", None),
        P(),
    )
    return jax.shard_map(
        per_device,
        mesh=fine,
        in_specs=placed,
        out_specs=(P(split, "gy", None), P(split, "gy", None), P(split, "gy", None), P()),
        check_vma=False,
    )
```

```python
import math

import jax
import jax.numpy as jnp
from jax import lax
from jax.sharding import PartitionSpec as P

BLOCK = 128
HEADS = 4


def with_halo(block, sides, width):
    for axis, dim in sides:
        count = lax.axis_size(axis)
        forward = [(i, i + 1) for i in range(count - 1)]
        forward.append((count - 1, 0))
        backward = [(target, source) for source, target in forward]
        low = lax.ppermute(
            lax.slice_in_dim(block, block.shape[dim] - width, None, axis=dim), axis, forward
        )
        high = lax.ppermute(lax.slice_in_dim(block, 0, width, axis=dim), axis, backward)
        block = jnp.concatenate([low, block, high], axis=dim)
    return block


def prime_factors(count):
    factors = []
    base = 2
    while count > 1:
        while count % base == 0:
            factors.append(base)
            count //= base
        base += 1
    return factors


def exchange_sum(value, axis):
    count = lax.axis_size(axis)
    index = lax.axis_index(axis)
    stride = 1
    for radix in prime_factors(count):
        digit = (index // stride) % radix
        if radix == 2:
            pairs = [(i, i + stride) if (i // stride) % 2 == 0 else (i, i - stride) for i in range(count)]
            value = value + lax.ppermute(value, axis, pairs)
        else:
            received = [value]
            for shift in range(1, radix):
                pairs = []
                for i in range(count):
                    d = (i // stride) % radix
                    pairs.append((i, i + (((d + shift) % radix) - d) * stride))
                received.append(lax.ppermute(value, axis, pairs))
            total = None
            for position in range(radix):
                offset = (digit - position) % radix
                term = received[0]
                for shift in range(1, radix):
                    term = jnp.where(offset == shift, received[shift], term)
                total = term if total is None else total + term
            value = total
        stride *= radix
    return value


def gather_sum(value, axis):
    count = lax.axis_size(axis)
    spread = jnp.broadcast_to(value[None], (count,) + value.shape)
    parts = lax.all_to_all(spread, axis, split_axis=0, concat_axis=0, tiled=True)
    return jnp.sum(parts, axis=0)


def tile_grads(row_pack, stat_pack, key_pack):
    features = row_pack.shape[3]
    head_width = features // HEADS
    softmax_scale = 1.0 / math.sqrt(head_width)
    head_of = jnp.arange(features, dtype=jnp.int32) // head_width
    mask = (head_of[None, :] == jnp.arange(HEADS, dtype=jnp.int32)[:, None]).astype(row_pack.dtype)

    def spread(part):
        return part[:, None] * mask[None, :, None, :]

    query_rows = row_pack[:, 0]
    grad_rows = row_pack[:, 1]
    key_rows = key_pack[:, 0]
    value_rows = key_pack[:, 1]
    query_heads = spread(query_rows)
    grad_heads = spread(grad_rows)
    key_heads = spread(key_rows)
    log_part = stat_pack[:, 0].astype(jnp.float32)
    delta_part = stat_pack[:, 1].astype(jnp.float32)
    scores = (
        jnp.einsum("shqf,skf->shqk", query_heads, key_rows, preferred_element_type=jnp.float32)
        * softmax_scale
    )
    weights = jnp.exp(scores - log_part[..., None])
    weight_grad = jnp.einsum(
        "shqf,skf->shqk", grad_heads, value_rows, preferred_element_type=jnp.float32
    )
    score_grad = weights * (weight_grad - delta_part[..., None])
    weights_low = weights.astype(jnp.bfloat16)
    score_low = score_grad.astype(jnp.bfloat16)
    value_part = jnp.einsum(
        "shqk,shqf->skf", weights_low, grad_heads, preferred_element_type=jnp.float32
    )
    key_part = (
        jnp.einsum("shqk,shqf->skf", score_low, query_heads, preferred_element_type=jnp.float32)
        * softmax_scale
    )
    query_part = (
        jnp.einsum("shqk,shkf->sqf", score_low, key_heads, preferred_element_type=jnp.float32)
        * softmax_scale
    )
    return (query_part, key_part, value_part)


def per_device(queries, keys, values, out_attn, out_grad, log_norm, neighbour_blocks, stencil):
    tile_x, tile_y, features = queries.shape
    row_blocks = tile_x * tile_y // BLOCK
    head_width = features // HEADS
    listed = neighbour_blocks.shape[2]
    group_size = lax.axis_size("gy")
    pair_count = row_blocks * listed
    capacity = max(2, (pair_count + group_size - 1) // group_size)
    slot_count = group_size * capacity
    query_blocks = queries.reshape(row_blocks, BLOCK, features)
    key_blocks = keys.reshape(row_blocks, BLOCK, features)
    value_blocks = values.reshape(row_blocks, BLOCK, features)
    grad_blocks = out_grad.reshape(row_blocks, BLOCK, features)
    products = out_grad.astype(jnp.float32) * out_attn.astype(jnp.float32)
    delta = products.reshape(row_blocks, BLOCK, HEADS, head_width).sum(-1).astype(jnp.bfloat16)
    delta = delta.transpose(0, 2, 1)
    norm_blocks = log_norm.reshape(HEADS, row_blocks, BLOCK).transpose(1, 0, 2)
    stat_blocks = jnp.stack([norm_blocks, delta], 1)
    row_pack = jnp.stack([query_blocks, grad_blocks], 1)
    key_pack = jnp.stack([key_blocks, value_blocks], 1)
    point_count = tile_x * tile_y * lax.axis_size("gx") * group_size
    columns = neighbour_blocks.reshape(pair_count)
    owners = columns // row_blocks
    inner = columns % row_blocks
    order = jnp.arange(pair_count, dtype=jnp.int32)
    before = (owners[:, None] == owners[None, :]) & (order[None, :] < order[:, None])
    rank = jnp.sum(before.astype(jnp.int32), 1)
    slot_of = owners * capacity + rank
    placed = (jnp.arange(slot_count, dtype=jnp.int32)[:, None] == slot_of[None, :]).astype(
        jnp.float32
    )
    source_rows = (
        (order // listed)[:, None] == jnp.arange(row_blocks, dtype=jnp.int32)[None, :]
    ).astype(jnp.float32)
    picker = jnp.dot(placed, source_rows, precision=lax.Precision.HIGHEST)
    picker_low = picker.astype(jnp.bfloat16)
    send_rows = jnp.dot(
        picker_low, row_pack.reshape(row_blocks, -1), preferred_element_type=jnp.float32
    )
    send_rows = send_rows.astype(jnp.bfloat16).reshape(group_size, capacity, 2, BLOCK, features)
    send_stats = jnp.dot(
        picker_low, stat_blocks.reshape(row_blocks, -1), preferred_element_type=jnp.float32
    )
    send_stats = send_stats.astype(jnp.bfloat16).reshape(group_size, capacity, 2, HEADS, BLOCK)
    send_ids = jnp.dot(placed, (inner + 1).astype(jnp.float32), precision=lax.Precision.HIGHEST)
    send_ids = send_ids.astype(jnp.bfloat16).reshape(group_size, capacity)
    stat_rows = send_stats.reshape(group_size, capacity, 2 * HEADS, BLOCK)
    id_rows = jnp.broadcast_to(send_ids[:, :, None, None], (group_size, capacity, 8, features))
    row_count = 2 * BLOCK
    send_pack = jnp.concatenate(
        [send_rows.reshape(group_size, capacity, row_count, features), stat_rows, id_rows], 2
    )
    slot_rows = send_pack.shape[2]
    send_pack = send_pack.reshape(group_size, capacity * slot_rows, features)
    send_pack, diag_rows, diag_stats, diag_keys, grad_x, values_x = lax.optimization_barrier(
        (send_pack, row_pack, stat_blocks, key_pack, out_grad, values)
    )
    pack_in = lax.all_to_all(send_pack, "gy", split_axis=0, concat_axis=0, tiled=True)
    count_x = lax.axis_size("gx")
    ahead = [(i, (i + 1) % count_x) for i in range(count_x)]
    behind = [((i + 1) % count_x, i) for i in range(count_x)]
    from_before = lax.ppermute(grad_x[tile_x - 1 :], "gx", ahead)
    from_after = lax.ppermute(grad_x[:1], "gx", behind)
    ahead_y = [(i, (i + 1) % group_size) for i in range(group_size)]
    behind_y = [((i + 1) % group_size, i) for i in range(group_size)]
    before_col = lax.ppermute(grad_x[:, tile_y - 1 :], "gy", ahead_y)
    after_col = lax.ppermute(grad_x[:, :1], "gy", behind_y)
    moved = [
        grad_x.astype(jnp.float32),
        jnp.concatenate([grad_x[1:], from_after], 0).astype(jnp.float32),
        jnp.concatenate([from_before, grad_x[:-1]], 0).astype(jnp.float32),
        jnp.concatenate([grad_x[:, 1:], after_col], 1).astype(jnp.float32),
        jnp.concatenate([before_col, grad_x[:, :-1]], 1).astype(jnp.float32),
    ]
    value_float = values_x.astype(jnp.float32)
    stencil_term = stencil[0] * moved[0]
    for index in range(1, 5):
        stencil_term = stencil_term + stencil[index] * moved[index]
    partial_rows = jnp.stack(
        [jnp.sum(moved[index] * value_float, axis=(0, 1)) for index in range(5)]
    )
    point_count = tile_x * tile_y * count_x * group_size
    column_sum = jnp.sum(lax.all_gather(partial_rows, "gx"), 0)
    diag_query, diag_key, diag_value = tile_grads(diag_rows, diag_stats, diag_keys)
    pack_in, diag_query, diag_key, diag_value, column_sum = lax.optimization_barrier(
        (pack_in, diag_query, diag_key, diag_value, column_sum)
    )
    pack_in = pack_in.reshape(group_size, capacity, slot_rows, features)
    rows_in = pack_in[:, :, :row_count].reshape(group_size, capacity, 2, BLOCK, features)
    stats_in = pack_in[:, :, row_count : row_count + 2 * HEADS].reshape(
        group_size, capacity, 2, HEADS, BLOCK
    )
    ids_in = pack_in[:, :, row_count + 2 * HEADS, 0]
    item_count = rows_in.shape[1]
    total_items = group_size * item_count
    wanted = ids_in.astype(jnp.float32).astype(jnp.int32) - 1
    chooser = (wanted[..., None] == jnp.arange(row_blocks, dtype=jnp.int32)).astype(jnp.bfloat16)
    keys_in = jnp.dot(
        chooser.reshape(-1, row_blocks),
        key_pack.reshape(row_blocks, -1),
        preferred_element_type=jnp.float32,
    )
    keys_in = keys_in.astype(jnp.bfloat16).reshape(total_items, 2, BLOCK, features)
    query_part, key_part, value_part = tile_grads(
        rows_in.reshape(total_items, 2, BLOCK, features),
        stats_in.reshape(total_items, 2, HEADS, BLOCK),
        keys_in,
    )
    query_part = query_part.reshape(group_size, item_count, BLOCK, features)
    key_part = key_part.reshape(group_size, item_count, BLOCK, features)
    value_part = value_part.reshape(group_size, item_count, BLOCK, features)
    stencil_count = partial_rows.shape[0]
    stencil_hi = column_sum.astype(jnp.bfloat16)
    stencil_rest = column_sum - stencil_hi.astype(jnp.float32)
    stencil_mid = stencil_rest.astype(jnp.bfloat16)
    stencil_lo = (stencil_rest - stencil_mid.astype(jnp.float32)).astype(jnp.bfloat16)
    stencil_terms = jnp.concatenate([stencil_hi, stencil_mid, stencil_lo], 0)
    term_rows = 3 * stencil_count
    stencil_pad = jnp.pad(stencil_terms, ((0, 16 - term_rows), (0, 0)))
    return_pack = jnp.concatenate(
        [
            query_part.reshape(group_size, item_count * BLOCK, features).astype(jnp.bfloat16),
            jnp.broadcast_to(stencil_pad[None], (group_size, 16, features)),
        ],
        1,
    )
    return_in = lax.all_to_all(return_pack, "gy", split_axis=0, concat_axis=0, tiled=True)
    returned = return_in[:, : item_count * BLOCK].astype(jnp.float32)
    terms_in = return_in[:, item_count * BLOCK : item_count * BLOCK + term_rows].astype(jnp.float32)
    terms_in = terms_in.reshape(group_size, 3, stencil_count, features)
    summed = jnp.sum(terms_in[:, 0] + terms_in[:, 1] + terms_in[:, 2], 0)
    returned, pieces, ids_in = (returned, jnp.stack([key_part, value_part], 2), ids_in)
    query_sum = diag_query + jnp.einsum(
        "sr,sbf->rbf",
        picker,
        returned.reshape(slot_count, BLOCK, features),
        precision=lax.Precision.HIGHEST,
    )
    arrived = ids_in.reshape(slot_count).astype(jnp.float32).astype(jnp.int32) - 1
    owned = (arrived[:, None] == jnp.arange(row_blocks, dtype=jnp.int32)[None, :]).astype(
        jnp.float32
    )
    key_value_sum = jnp.einsum(
        "sr,sxbf->rxbf",
        owned,
        pieces.reshape(slot_count, 2, BLOCK, features),
        precision=lax.Precision.HIGHEST,
    )
    key_total = diag_key + key_value_sum[:, 0]
    value_total = diag_value + key_value_sum[:, 1]
    stencil_grad = summed / math.sqrt(point_count)
    query_grad = query_sum.reshape(tile_x, tile_y, features).astype(jnp.bfloat16)
    key_grad = key_total.reshape(tile_x, tile_y, features).astype(jnp.bfloat16)
    value_grad = (value_total.reshape(tile_x, tile_y, features) + stencil_term).astype(jnp.bfloat16)
    return (query_grad, key_grad, value_grad, stencil_grad)


def solution(mesh):
    placed = (
        P("gx", "gy", None),
        P("gx", "gy", None),
        P("gx", "gy", None),
        P("gx", "gy", None),
        P("gx", "gy", None),
        P(None, "gx", "gy"),
        P("gx", "gy", None),
        P(),
    )
    return jax.shard_map(
        per_device,
        mesh=mesh,
        in_specs=placed,
        out_specs=(P("gx", "gy", None), P("gx", "gy", None), P("gx", "gy", None), P()),
        check_vma=False,
    )
```

```python
import math

import jax
import jax.numpy as jnp
from jax import lax
from jax.sharding import PartitionSpec as P

BLOCK = 128
HEADS = 4


def with_halo(block, sides, width):
    for axis, dim in sides:
        count = lax.axis_size(axis)
        forward = [(i, i + 1) for i in range(count - 1)]
        forward.append((count - 1, 0))
        backward = [(target, source) for source, target in forward]
        low = lax.ppermute(
            lax.slice_in_dim(block, block.shape[dim] - width, None, axis=dim), axis, forward
        )
        high = lax.ppermute(lax.slice_in_dim(block, 0, width, axis=dim), axis, backward)
        block = jnp.concatenate([low, block, high], axis=dim)
    return block


def prime_factors(count):
    factors = []
    base = 2
    while count > 1:
        while count % base == 0:
            factors.append(base)
            count //= base
        base += 1
    return factors


def exchange_sum(value, axis):
    count = lax.axis_size(axis)
    index = lax.axis_index(axis)
    stride = 1
    for radix in prime_factors(count):
        digit = (index // stride) % radix
        if radix == 2:
            pairs = [(i, i + stride) if (i // stride) % 2 == 0 else (i, i - stride) for i in range(count)]
            value = value + lax.ppermute(value, axis, pairs)
        else:
            received = [value]
            for shift in range(1, radix):
                pairs = []
                for i in range(count):
                    d = (i // stride) % radix
                    pairs.append((i, i + (((d + shift) % radix) - d) * stride))
                received.append(lax.ppermute(value, axis, pairs))
            total = None
            for position in range(radix):
                offset = (digit - position) % radix
                term = received[0]
                for shift in range(1, radix):
                    term = jnp.where(offset == shift, received[shift], term)
                total = term if total is None else total + term
            value = total
        stride *= radix
    return value


def gather_sum(value, axis):
    count = lax.axis_size(axis)
    spread = jnp.broadcast_to(value[None], (count,) + value.shape)
    parts = lax.all_to_all(spread, axis, split_axis=0, concat_axis=0, tiled=True)
    return jnp.sum(parts, axis=0)


def tile_grads(row_pack, stat_pack, key_pack):
    features = row_pack.shape[3]
    head_width = features // HEADS
    softmax_scale = 1.0 / math.sqrt(head_width)
    head_of = jnp.arange(features, dtype=jnp.int32) // head_width
    mask = (head_of[None, :] == jnp.arange(HEADS, dtype=jnp.int32)[:, None]).astype(row_pack.dtype)

    def spread(part):
        return part[:, None] * mask[None, :, None, :]

    query_rows = row_pack[:, 0]
    grad_rows = row_pack[:, 1]
    key_rows = key_pack[:, 0]
    value_rows = key_pack[:, 1]
    query_heads = spread(query_rows)
    grad_heads = spread(grad_rows)
    key_heads = spread(key_rows)
    log_part = stat_pack[:, 0].astype(jnp.float32)
    delta_part = stat_pack[:, 1].astype(jnp.float32)
    scores = (
        jnp.einsum("shqf,skf->shqk", query_heads, key_rows, preferred_element_type=jnp.float32)
        * softmax_scale
    )
    weights = jnp.exp(scores - log_part[..., None])
    weight_grad = jnp.einsum(
        "shqf,skf->shqk", grad_heads, value_rows, preferred_element_type=jnp.float32
    )
    score_grad = weights * (weight_grad - delta_part[..., None])
    weights_low = weights.astype(jnp.bfloat16)
    score_low = score_grad.astype(jnp.bfloat16)
    value_part = jnp.einsum(
        "shqk,shqf->skf", weights_low, grad_heads, preferred_element_type=jnp.float32
    )
    key_part = (
        jnp.einsum("shqk,shqf->skf", score_low, query_heads, preferred_element_type=jnp.float32)
        * softmax_scale
    )
    query_part = (
        jnp.einsum("shqk,shkf->sqf", score_low, key_heads, preferred_element_type=jnp.float32)
        * softmax_scale
    )
    return (query_part, key_part, value_part)


def per_device(queries, keys, values, out_attn, out_grad, log_norm, neighbour_blocks, stencil):
    tile_x, tile_y, features = queries.shape
    row_blocks = tile_x * tile_y // BLOCK
    head_width = features // HEADS
    listed = neighbour_blocks.shape[2]
    group_size = lax.axis_size("gy")
    pair_count = row_blocks * listed
    capacity = max(2, (pair_count + group_size - 1) // group_size)
    slot_count = group_size * capacity
    query_blocks = queries.reshape(row_blocks, BLOCK, features)
    key_blocks = keys.reshape(row_blocks, BLOCK, features)
    value_blocks = values.reshape(row_blocks, BLOCK, features)
    grad_blocks = out_grad.reshape(row_blocks, BLOCK, features)
    products = out_grad.astype(jnp.float32) * out_attn.astype(jnp.float32)
    delta = products.reshape(row_blocks, BLOCK, HEADS, head_width).sum(-1).astype(jnp.bfloat16)
    delta = delta.transpose(0, 2, 1)
    norm_blocks = log_norm.reshape(HEADS, row_blocks, BLOCK).transpose(1, 0, 2)
    stat_blocks = jnp.stack([norm_blocks, delta], 1)
    row_pack = jnp.stack([query_blocks, grad_blocks], 1)
    key_pack = jnp.stack([key_blocks, value_blocks], 1)
    point_count = tile_x * tile_y * lax.axis_size("gx") * group_size
    columns = neighbour_blocks.reshape(pair_count)
    owners = columns // row_blocks
    inner = columns % row_blocks
    order = jnp.arange(pair_count, dtype=jnp.int32)
    before = (owners[:, None] == owners[None, :]) & (order[None, :] < order[:, None])
    rank = jnp.sum(before.astype(jnp.int32), 1)
    slot_of = owners * capacity + rank
    placed = (jnp.arange(slot_count, dtype=jnp.int32)[:, None] == slot_of[None, :]).astype(
        jnp.float32
    )
    source_rows = (
        (order // listed)[:, None] == jnp.arange(row_blocks, dtype=jnp.int32)[None, :]
    ).astype(jnp.float32)
    picker = jnp.dot(placed, source_rows, precision=lax.Precision.HIGHEST)
    picker_low = picker.astype(jnp.bfloat16)
    source_index = jnp.dot(
        placed, (order // listed + 1).astype(jnp.float32), precision=lax.Precision.HIGHEST
    ).astype(jnp.int32) - 1
    source_index = jnp.where(source_index < 0, row_blocks, source_index)
    source_pack = jnp.concatenate(
        [row_pack.reshape(row_blocks, 2 * BLOCK, features), stat_blocks.reshape(row_blocks, -1, BLOCK)],
        1,
    )
    source_pack = jnp.pad(source_pack, ((0, 1), (0, 0), (0, 0)))
    send_pack = jnp.take(source_pack, source_index, axis=0)
    send_ids = jnp.dot(placed, (inner + 1).astype(jnp.float32), precision=lax.Precision.HIGHEST)
    send_ids = send_ids.astype(jnp.bfloat16).reshape(group_size, capacity)
    id_rows = jnp.broadcast_to(send_ids[:, :, None, None], (group_size, capacity, 8, features))
    row_count = 2 * BLOCK
    send_pack = jnp.concatenate(
        [send_pack.reshape(group_size, capacity, -1, features), id_rows], 2
    )
    slot_rows = send_pack.shape[2]
    edges = jnp.concatenate([out_grad[:, 0], out_grad[:, tile_y - 1]], 0)
    send_pack = jnp.concatenate(
        [
            send_pack.reshape(group_size, capacity * slot_rows, features),
            jnp.broadcast_to(edges[None], (group_size,) + edges.shape),
        ],
        1,
    )
    send_pack, diag_rows, diag_stats, diag_keys = lax.optimization_barrier(
        (send_pack, row_pack, stat_blocks, key_pack)
    )
    pack_in = lax.all_to_all(send_pack, "gy", split_axis=0, concat_axis=0, tiled=True)
    diag_query, diag_key, diag_value = tile_grads(diag_rows, diag_stats, diag_keys)
    pack_in, diag_query, diag_key, diag_value = lax.optimization_barrier(
        (pack_in, diag_query, diag_key, diag_value)
    )
    column = lax.axis_index("gy")
    edge_in = pack_in[:, capacity * slot_rows :]
    before_col = lax.dynamic_index_in_dim(edge_in, (column + group_size - 1) % group_size, 0, False)
    after_col = lax.dynamic_index_in_dim(edge_in, (column + 1) % group_size, 0, False)
    before_col = before_col[tile_x:]
    after_col = after_col[:tile_x]
    grad_x, values_x = lax.optimization_barrier((out_grad, values))
    count_x = lax.axis_size("gx")
    ahead = [(i, (i + 1) % count_x) for i in range(count_x)]
    behind = [((i + 1) % count_x, i) for i in range(count_x)]
    from_before = lax.ppermute(grad_x[tile_x - 1 :], "gx", ahead)
    from_after = lax.ppermute(grad_x[:1], "gx", behind)
    moved = [
        grad_x.astype(jnp.float32),
        jnp.concatenate([grad_x[1:], from_after], 0).astype(jnp.float32),
        jnp.concatenate([from_before, grad_x[:-1]], 0).astype(jnp.float32),
        jnp.concatenate([grad_x[:, 1:], after_col[:, None]], 1).astype(jnp.float32),
        jnp.concatenate([before_col[:, None], grad_x[:, :-1]], 1).astype(jnp.float32),
    ]
    value_float = values_x.astype(jnp.float32)
    stencil_term = stencil[0] * moved[0]
    for index in range(1, 5):
        stencil_term = stencil_term + stencil[index] * moved[index]
    partial_rows = jnp.stack(
        [jnp.sum(moved[index] * value_float, axis=(0, 1)) for index in range(5)]
    )
    point_count = tile_x * tile_y * count_x * group_size
    pack_in = pack_in[:, : capacity * slot_rows].reshape(group_size, capacity, slot_rows, features)
    partial_rows, pack_in = lax.optimization_barrier((partial_rows, pack_in))
    column_sum = gather_sum(partial_rows, "gx")
    rows_in = pack_in[:, :, :row_count].reshape(group_size, capacity, 2, BLOCK, features)
    stats_in = pack_in[:, :, row_count : row_count + 2 * HEADS].reshape(
        group_size, capacity, 2, HEADS, BLOCK
    )
    ids_in = pack_in[:, :, row_count + 2 * HEADS, 0]
    item_count = rows_in.shape[1]
    total_items = group_size * item_count
    wanted = ids_in.astype(jnp.float32).astype(jnp.int32) - 1
    key_index = jnp.where(wanted < 0, row_blocks, wanted).reshape(-1)
    keys_in = jnp.take(jnp.pad(key_pack, ((0, 1), (0, 0), (0, 0), (0, 0))), key_index, axis=0)
    keys_in = keys_in.astype(jnp.bfloat16).reshape(total_items, 2, BLOCK, features)
    query_part, key_part, value_part = tile_grads(
        rows_in.reshape(total_items, 2, BLOCK, features),
        stats_in.reshape(total_items, 2, HEADS, BLOCK),
        keys_in,
    )
    query_part = query_part.reshape(group_size, item_count, BLOCK, features)
    key_part = key_part.reshape(group_size, item_count, BLOCK, features)
    value_part = value_part.reshape(group_size, item_count, BLOCK, features)
    stencil_count = partial_rows.shape[0]
    stencil_hi = column_sum.astype(jnp.bfloat16)
    stencil_rest = column_sum - stencil_hi.astype(jnp.float32)
    stencil_mid = stencil_rest.astype(jnp.bfloat16)
    stencil_lo = (stencil_rest - stencil_mid.astype(jnp.float32)).astype(jnp.bfloat16)
    stencil_terms = jnp.concatenate([stencil_hi, stencil_mid, stencil_lo], 0)
    term_rows = 3 * stencil_count
    stencil_pad = jnp.pad(stencil_terms, ((0, 16 - term_rows), (0, 0)))
    return_pack = jnp.concatenate(
        [
            query_part.reshape(group_size, item_count * BLOCK, features).astype(jnp.bfloat16),
            jnp.broadcast_to(stencil_pad[None], (group_size, 16, features)),
        ],
        1,
    )
    return_in = lax.all_to_all(return_pack, "gy", split_axis=0, concat_axis=0, tiled=True)
    returned = return_in[:, : item_count * BLOCK].astype(jnp.float32)
    terms_in = return_in[:, item_count * BLOCK : item_count * BLOCK + term_rows].astype(jnp.float32)
    terms_in = terms_in.reshape(group_size, 3, stencil_count, features)
    summed = jnp.sum(terms_in[:, 0] + terms_in[:, 1] + terms_in[:, 2], 0)
    returned, pieces, ids_in = (returned, jnp.stack([key_part, value_part], 2), ids_in)
    query_sum = diag_query + jnp.einsum(
        "sr,sbf->rbf",
        picker,
        returned.reshape(slot_count, BLOCK, features),
        precision=lax.Precision.HIGHEST,
    )
    arrived = ids_in.reshape(slot_count).astype(jnp.float32).astype(jnp.int32) - 1
    owned = (arrived[:, None] == jnp.arange(row_blocks, dtype=jnp.int32)[None, :]).astype(
        jnp.float32
    )
    key_value_sum = jnp.einsum(
        "sr,sxbf->rxbf",
        owned,
        pieces.reshape(slot_count, 2, BLOCK, features),
        precision=lax.Precision.HIGHEST,
    )
    key_total = diag_key + key_value_sum[:, 0]
    value_total = diag_value + key_value_sum[:, 1]
    stencil_grad = summed / math.sqrt(point_count)
    query_grad = query_sum.reshape(tile_x, tile_y, features).astype(jnp.bfloat16)
    key_grad = key_total.reshape(tile_x, tile_y, features).astype(jnp.bfloat16)
    value_grad = (value_total.reshape(tile_x, tile_y, features) + stencil_term).astype(jnp.bfloat16)
    return (query_grad, key_grad, value_grad, stencil_grad)


def solution(mesh):
    placed = (
        P("gx", "gy", None),
        P("gx", "gy", None),
        P("gx", "gy", None),
        P("gx", "gy", None),
        P("gx", "gy", None),
        P(None, "gx", "gy"),
        P("gx", "gy", None),
        P(),
    )
    return jax.shard_map(
        per_device,
        mesh=mesh,
        in_specs=placed,
        out_specs=(P("gx", "gy", None), P("gx", "gy", None), P("gx", "gy", None), P()),
        check_vma=False,
    )
```

```python
import math

import jax
import jax.numpy as jnp
from jax import lax
from jax.sharding import PartitionSpec as P

BLOCK = 128
HEADS = 4


def with_halo(block, sides, width):
    for axis, dim in sides:
        count = lax.axis_size(axis)
        forward = [(i, i + 1) for i in range(count - 1)]
        forward.append((count - 1, 0))
        backward = [(target, source) for source, target in forward]
        low = lax.ppermute(
            lax.slice_in_dim(block, block.shape[dim] - width, None, axis=dim), axis, forward
        )
        high = lax.ppermute(lax.slice_in_dim(block, 0, width, axis=dim), axis, backward)
        block = jnp.concatenate([low, block, high], axis=dim)
    return block


def prime_factors(count):
    factors = []
    base = 2
    while count > 1:
        while count % base == 0:
            factors.append(base)
            count //= base
        base += 1
    return factors


def exchange_sum(value, axis):
    count = lax.axis_size(axis)
    index = lax.axis_index(axis)
    stride = 1
    for radix in prime_factors(count):
        digit = (index // stride) % radix
        if radix == 2:
            pairs = [(i, i + stride) if (i // stride) % 2 == 0 else (i, i - stride) for i in range(count)]
            value = value + lax.ppermute(value, axis, pairs)
        else:
            received = [value]
            for shift in range(1, radix):
                pairs = []
                for i in range(count):
                    d = (i // stride) % radix
                    pairs.append((i, i + (((d + shift) % radix) - d) * stride))
                received.append(lax.ppermute(value, axis, pairs))
            total = None
            for position in range(radix):
                offset = (digit - position) % radix
                term = received[0]
                for shift in range(1, radix):
                    term = jnp.where(offset == shift, received[shift], term)
                total = term if total is None else total + term
            value = total
        stride *= radix
    return value


def gather_sum(value, axis):
    count = lax.axis_size(axis)
    spread = jnp.broadcast_to(value[None], (count,) + value.shape)
    parts = lax.all_to_all(spread, axis, split_axis=0, concat_axis=0, tiled=True)
    return jnp.sum(parts, axis=0)


def tile_grads(row_pack, stat_pack, key_pack):
    features = row_pack.shape[3]
    head_width = features // HEADS
    softmax_scale = 1.0 / math.sqrt(head_width)
    head_of = jnp.arange(features, dtype=jnp.int32) // head_width
    mask = (head_of[None, :] == jnp.arange(HEADS, dtype=jnp.int32)[:, None]).astype(row_pack.dtype)

    def spread(part):
        return part[:, None] * mask[None, :, None, :]

    query_rows = row_pack[:, 0]
    grad_rows = row_pack[:, 1]
    key_rows = key_pack[:, 0]
    value_rows = key_pack[:, 1]
    query_heads = spread(query_rows)
    grad_heads = spread(grad_rows)
    key_heads = spread(key_rows)
    log_part = stat_pack[:, 0].astype(jnp.float32)
    delta_part = stat_pack[:, 1].astype(jnp.float32)
    scores = (
        jnp.einsum("shqf,skf->shqk", query_heads, key_rows, preferred_element_type=jnp.float32)
        * softmax_scale
    )
    weights = jnp.exp(scores - log_part[..., None])
    weight_grad = jnp.einsum(
        "shqf,skf->shqk", grad_heads, value_rows, preferred_element_type=jnp.float32
    )
    score_grad = weights * (weight_grad - delta_part[..., None])
    weights_low = weights.astype(jnp.bfloat16)
    score_low = score_grad.astype(jnp.bfloat16)
    value_part = jnp.einsum(
        "shqk,shqf->skf", weights_low, grad_heads, preferred_element_type=jnp.float32
    )
    key_part = (
        jnp.einsum("shqk,shqf->skf", score_low, query_heads, preferred_element_type=jnp.float32)
        * softmax_scale
    )
    query_part = (
        jnp.einsum("shqk,shkf->sqf", score_low, key_heads, preferred_element_type=jnp.float32)
        * softmax_scale
    )
    return (query_part, key_part, value_part)


def per_device(queries, keys, values, out_attn, out_grad, log_norm, neighbour_blocks, stencil):
    tile_x, tile_y, features = queries.shape
    row_blocks = tile_x * tile_y // BLOCK
    head_width = features // HEADS
    listed = neighbour_blocks.shape[2]
    group_size = lax.axis_size("gy")
    pair_count = row_blocks * listed
    capacity = max(2, (pair_count + group_size - 1) // group_size)
    slot_count = group_size * capacity
    query_blocks = queries.reshape(row_blocks, BLOCK, features)
    key_blocks = keys.reshape(row_blocks, BLOCK, features)
    value_blocks = values.reshape(row_blocks, BLOCK, features)
    grad_blocks = out_grad.reshape(row_blocks, BLOCK, features)
    products = out_grad.astype(jnp.float32) * out_attn.astype(jnp.float32)
    delta = products.reshape(row_blocks, BLOCK, HEADS, head_width).sum(-1).astype(jnp.bfloat16)
    delta = delta.transpose(0, 2, 1)
    norm_blocks = log_norm.reshape(HEADS, row_blocks, BLOCK).transpose(1, 0, 2)
    stat_blocks = jnp.stack([norm_blocks, delta], 1)
    row_pack = jnp.stack([query_blocks, grad_blocks], 1)
    key_pack = jnp.stack([key_blocks, value_blocks], 1)
    point_count = tile_x * tile_y * lax.axis_size("gx") * group_size
    columns = neighbour_blocks.reshape(pair_count)
    owners = columns // row_blocks
    inner = columns % row_blocks
    order = jnp.arange(pair_count, dtype=jnp.int32)
    before = (owners[:, None] == owners[None, :]) & (order[None, :] < order[:, None])
    rank = jnp.sum(before.astype(jnp.int32), 1)
    slot_of = owners * capacity + rank
    placed = (jnp.arange(slot_count, dtype=jnp.int32)[:, None] == slot_of[None, :]).astype(
        jnp.float32
    )
    source_rows = (
        (order // listed)[:, None] == jnp.arange(row_blocks, dtype=jnp.int32)[None, :]
    ).astype(jnp.float32)
    picker = jnp.dot(placed, source_rows, precision=lax.Precision.HIGHEST)
    picker_low = picker.astype(jnp.bfloat16)
    send_rows = jnp.dot(
        picker_low, row_pack.reshape(row_blocks, -1), preferred_element_type=jnp.float32
    )
    send_rows = send_rows.astype(jnp.bfloat16).reshape(group_size, capacity, 2, BLOCK, features)
    send_stats = jnp.dot(
        picker_low, stat_blocks.reshape(row_blocks, -1), preferred_element_type=jnp.float32
    )
    send_stats = send_stats.astype(jnp.bfloat16).reshape(group_size, capacity, 2, HEADS, BLOCK)
    send_ids = jnp.dot(placed, (inner + 1).astype(jnp.float32), precision=lax.Precision.HIGHEST)
    send_ids = send_ids.astype(jnp.bfloat16).reshape(group_size, capacity)
    stat_rows = send_stats.reshape(group_size, capacity, 2 * HEADS, BLOCK)
    id_rows = jnp.broadcast_to(send_ids[:, :, None, None], (group_size, capacity, 8, features))
    row_count = 2 * BLOCK
    send_pack = jnp.concatenate(
        [send_rows.reshape(group_size, capacity, row_count, features), stat_rows, id_rows], 2
    )
    slot_rows = send_pack.shape[2]
    send_pack = send_pack.reshape(group_size, capacity * slot_rows, features)
    send_pack, diag_rows, diag_stats, diag_keys, grad_x, values_x = lax.optimization_barrier(
        (send_pack, row_pack, stat_blocks, key_pack, out_grad, values)
    )
    pack_in = lax.all_to_all(send_pack, "gy", split_axis=0, concat_axis=0, tiled=True)
    count_x = lax.axis_size("gx")
    ahead = [(i, (i + 1) % count_x) for i in range(count_x)]
    behind = [((i + 1) % count_x, i) for i in range(count_x)]
    from_before = lax.ppermute(grad_x[tile_x - 1 :], "gx", ahead)
    from_after = lax.ppermute(grad_x[:1], "gx", behind)
    ahead_y = [(i, (i + 1) % group_size) for i in range(group_size)]
    behind_y = [((i + 1) % group_size, i) for i in range(group_size)]
    before_col = lax.ppermute(grad_x[:, tile_y - 1 :], "gy", ahead_y)
    after_col = lax.ppermute(grad_x[:, :1], "gy", behind_y)
    moved = [
        grad_x.astype(jnp.float32),
        jnp.concatenate([grad_x[1:], from_after], 0).astype(jnp.float32),
        jnp.concatenate([from_before, grad_x[:-1]], 0).astype(jnp.float32),
        jnp.concatenate([grad_x[:, 1:], after_col], 1).astype(jnp.float32),
        jnp.concatenate([before_col, grad_x[:, :-1]], 1).astype(jnp.float32),
    ]
    value_float = values_x.astype(jnp.float32)
    stencil_term = stencil[0] * moved[0]
    for index in range(1, 5):
        stencil_term = stencil_term + stencil[index] * moved[index]
    partial_rows = jnp.stack(
        [jnp.sum(moved[index] * value_float, axis=(0, 1)) for index in range(5)]
    )
    point_count = tile_x * tile_y * count_x * group_size
    column_sum = exchange_sum(partial_rows, "gx")
    diag_query, diag_key, diag_value = tile_grads(diag_rows, diag_stats, diag_keys)
    pack_in, diag_query, diag_key, diag_value, column_sum = lax.optimization_barrier(
        (pack_in, diag_query, diag_key, diag_value, column_sum)
    )
    pack_in = pack_in.reshape(group_size, capacity, slot_rows, features)
    rows_in = pack_in[:, :, :row_count].reshape(group_size, capacity, 2, BLOCK, features)
    stats_in = pack_in[:, :, row_count : row_count + 2 * HEADS].reshape(
        group_size, capacity, 2, HEADS, BLOCK
    )
    ids_in = pack_in[:, :, row_count + 2 * HEADS, 0]
    item_count = rows_in.shape[1]
    total_items = group_size * item_count
    wanted = ids_in.astype(jnp.float32).astype(jnp.int32) - 1
    chooser = (wanted[..., None] == jnp.arange(row_blocks, dtype=jnp.int32)).astype(jnp.bfloat16)
    keys_in = jnp.dot(
        chooser.reshape(-1, row_blocks),
        key_pack.reshape(row_blocks, -1),
        preferred_element_type=jnp.float32,
    )
    keys_in = keys_in.astype(jnp.bfloat16).reshape(total_items, 2, BLOCK, features)
    query_part, key_part, value_part = tile_grads(
        rows_in.reshape(total_items, 2, BLOCK, features),
        stats_in.reshape(total_items, 2, HEADS, BLOCK),
        keys_in,
    )
    query_part = query_part.reshape(group_size, item_count, BLOCK, features)
    key_part = key_part.reshape(group_size, item_count, BLOCK, features)
    value_part = value_part.reshape(group_size, item_count, BLOCK, features)
    stencil_count = partial_rows.shape[0]
    stencil_hi = column_sum.astype(jnp.bfloat16)
    stencil_rest = column_sum - stencil_hi.astype(jnp.float32)
    stencil_mid = stencil_rest.astype(jnp.bfloat16)
    stencil_lo = (stencil_rest - stencil_mid.astype(jnp.float32)).astype(jnp.bfloat16)
    stencil_terms = jnp.concatenate([stencil_hi, stencil_mid, stencil_lo], 0)
    term_rows = 3 * stencil_count
    stencil_pad = jnp.pad(stencil_terms, ((0, 16 - term_rows), (0, 0)))
    return_pack = jnp.concatenate(
        [
            query_part.reshape(group_size, item_count * BLOCK, features).astype(jnp.bfloat16),
            jnp.broadcast_to(stencil_pad[None], (group_size, 16, features)),
        ],
        1,
    )
    return_in = lax.all_to_all(return_pack, "gy", split_axis=0, concat_axis=0, tiled=True)
    returned = return_in[:, : item_count * BLOCK].astype(jnp.float32)
    terms_in = return_in[:, item_count * BLOCK : item_count * BLOCK + term_rows].astype(jnp.float32)
    terms_in = terms_in.reshape(group_size, 3, stencil_count, features)
    summed = jnp.sum(terms_in[:, 0] + terms_in[:, 1] + terms_in[:, 2], 0)
    returned, pieces, ids_in = (returned, jnp.stack([key_part, value_part], 2), ids_in)
    query_sum = diag_query + jnp.einsum(
        "sr,sbf->rbf",
        picker,
        returned.reshape(slot_count, BLOCK, features),
        precision=lax.Precision.HIGHEST,
    )
    arrived = ids_in.reshape(slot_count).astype(jnp.float32).astype(jnp.int32) - 1
    owned = (arrived[:, None] == jnp.arange(row_blocks, dtype=jnp.int32)[None, :]).astype(
        jnp.float32
    )
    key_value_sum = jnp.einsum(
        "sr,sxbf->rxbf",
        owned,
        pieces.reshape(slot_count, 2, BLOCK, features),
        precision=lax.Precision.HIGHEST,
    )
    key_total = diag_key + key_value_sum[:, 0]
    value_total = diag_value + key_value_sum[:, 1]
    stencil_grad = summed / math.sqrt(point_count)
    query_grad = query_sum.reshape(tile_x, tile_y, features).astype(jnp.bfloat16)
    key_grad = key_total.reshape(tile_x, tile_y, features).astype(jnp.bfloat16)
    value_grad = (value_total.reshape(tile_x, tile_y, features) + stencil_term).astype(jnp.bfloat16)
    return (query_grad, key_grad, value_grad, stencil_grad)


def solution(mesh):
    placed = (
        P("gx", "gy", None),
        P("gx", "gy", None),
        P("gx", "gy", None),
        P("gx", "gy", None),
        P("gx", "gy", None),
        P(None, "gx", "gy"),
        P("gx", "gy", None),
        P(),
    )
    return jax.shard_map(
        per_device,
        mesh=mesh,
        in_specs=placed,
        out_specs=(P("gx", "gy", None), P("gx", "gy", None), P("gx", "gy", None), P()),
        check_vma=False,
    )
```

```python
import math

import jax
import jax.numpy as jnp
from jax import lax
from jax.sharding import PartitionSpec as P

BLOCK = 128
HEADS = 4
OUTER = "gx_outer"
INNER = "gx_inner"
PLANE = 8


def prime_factors(count):
    factors = []
    base = 2
    while count > 1:
        while count % base == 0:
            factors.append(base)
            count //= base
        base += 1
    return factors


def exchange_sum(value, axis):
    count = lax.axis_size(axis)
    index = lax.axis_index(axis)
    stride = 1
    for radix in prime_factors(count):
        digit = (index // stride) % radix
        if radix == 2:
            pairs = [(i, i + stride) if (i // stride) % 2 == 0 else (i, i - stride) for i in range(count)]
            value = value + lax.ppermute(value, axis, pairs)
        else:
            received = [value]
            for shift in range(1, radix):
                pairs = []
                for i in range(count):
                    d = (i // stride) % radix
                    pairs.append((i, i + (((d + shift) % radix) - d) * stride))
                received.append(lax.ppermute(value, axis, pairs))
            total = None
            for position in range(radix):
                offset = (digit - position) % radix
                term = received[0]
                for shift in range(1, radix):
                    term = jnp.where(offset == shift, received[shift], term)
                total = term if total is None else total + term
            value = total
        stride *= radix
    return value


def gather_sum(value, axis):
    count = lax.axis_size(axis)
    spread = jnp.broadcast_to(value[None], (count,) + value.shape)
    parts = lax.all_to_all(spread, axis, split_axis=0, concat_axis=0, tiled=True)
    return jnp.sum(parts, axis=0)


def tile_grads(row_pack, stat_pack, key_pack):
    features = row_pack.shape[3]
    head_width = features // HEADS
    softmax_scale = 1.0 / math.sqrt(head_width)
    head_of = jnp.arange(features, dtype=jnp.int32) // head_width
    mask = (head_of[None, :] == jnp.arange(HEADS, dtype=jnp.int32)[:, None]).astype(row_pack.dtype)

    def spread(part):
        return part[:, None] * mask[None, :, None, :]

    query_rows = row_pack[:, 0]
    grad_rows = row_pack[:, 1]
    key_rows = key_pack[:, 0]
    value_rows = key_pack[:, 1]
    query_heads = spread(query_rows)
    grad_heads = spread(grad_rows)
    key_heads = spread(key_rows)
    log_part = stat_pack[:, 0].astype(jnp.float32)
    delta_part = stat_pack[:, 1].astype(jnp.float32)
    scores = (
        jnp.einsum("shqf,skf->shqk", query_heads, key_rows, preferred_element_type=jnp.float32)
        * softmax_scale
    )
    weights = jnp.exp(scores - log_part[..., None])
    weight_grad = jnp.einsum(
        "shqf,skf->shqk", grad_heads, value_rows, preferred_element_type=jnp.float32
    )
    score_grad = weights * (weight_grad - delta_part[..., None])
    weights_low = weights.astype(jnp.bfloat16)
    score_low = score_grad.astype(jnp.bfloat16)
    value_part = jnp.einsum(
        "shqk,shqf->skf", weights_low, grad_heads, preferred_element_type=jnp.float32
    )
    key_part = (
        jnp.einsum("shqk,shqf->skf", score_low, query_heads, preferred_element_type=jnp.float32)
        * softmax_scale
    )
    query_part = (
        jnp.einsum("shqk,shkf->sqf", score_low, key_heads, preferred_element_type=jnp.float32)
        * softmax_scale
    )
    return (query_part, key_part, value_part)


def per_device(queries, keys, values, out_attn, out_grad, log_norm, neighbour_blocks, stencil):
    tile_x, tile_y, features = queries.shape
    row_blocks = tile_x * tile_y // BLOCK
    head_width = features // HEADS
    listed = neighbour_blocks.shape[2]
    group_size = lax.axis_size("gy")
    pair_count = row_blocks * listed
    capacity = max(2, (pair_count + group_size - 1) // group_size)
    slot_count = group_size * capacity
    query_blocks = queries.reshape(row_blocks, BLOCK, features)
    key_blocks = keys.reshape(row_blocks, BLOCK, features)
    value_blocks = values.reshape(row_blocks, BLOCK, features)
    grad_blocks = out_grad.reshape(row_blocks, BLOCK, features)
    products = out_grad.astype(jnp.float32) * out_attn.astype(jnp.float32)
    delta = products.reshape(row_blocks, BLOCK, HEADS, head_width).sum(-1).astype(jnp.bfloat16)
    delta = delta.transpose(0, 2, 1)
    norm_blocks = log_norm.reshape(HEADS, row_blocks, BLOCK).transpose(1, 0, 2)
    stat_blocks = jnp.stack([norm_blocks, delta], 1)
    row_pack = jnp.stack([query_blocks, grad_blocks], 1)
    key_pack = jnp.stack([key_blocks, value_blocks], 1)
    point_count = tile_x * tile_y * (lax.axis_size(OUTER) * lax.axis_size(INNER)) * group_size
    columns = neighbour_blocks.reshape(pair_count)
    owners = columns // row_blocks
    inner = columns % row_blocks
    order = jnp.arange(pair_count, dtype=jnp.int32)
    before = (owners[:, None] == owners[None, :]) & (order[None, :] < order[:, None])
    rank = jnp.sum(before.astype(jnp.int32), 1)
    slot_of = owners * capacity + rank
    placed = (jnp.arange(slot_count, dtype=jnp.int32)[:, None] == slot_of[None, :]).astype(
        jnp.float32
    )
    source_rows = (
        (order // listed)[:, None] == jnp.arange(row_blocks, dtype=jnp.int32)[None, :]
    ).astype(jnp.float32)
    picker = jnp.dot(placed, source_rows, precision=lax.Precision.HIGHEST)
    picker_low = picker.astype(jnp.bfloat16)
    send_rows = jnp.dot(
        picker_low, row_pack.reshape(row_blocks, -1), preferred_element_type=jnp.float32
    )
    send_rows = send_rows.astype(jnp.bfloat16).reshape(group_size, capacity, 2, BLOCK, features)
    send_stats = jnp.dot(
        picker_low, stat_blocks.reshape(row_blocks, -1), preferred_element_type=jnp.float32
    )
    send_stats = send_stats.astype(jnp.bfloat16).reshape(group_size, capacity, 2, HEADS, BLOCK)
    send_ids = jnp.dot(placed, (inner + 1).astype(jnp.float32), precision=lax.Precision.HIGHEST)
    send_ids = send_ids.astype(jnp.bfloat16).reshape(group_size, capacity)
    stat_rows = send_stats.reshape(group_size, capacity, 2 * HEADS, BLOCK)
    id_rows = jnp.broadcast_to(send_ids[:, :, None, None], (group_size, capacity, 8, features))
    row_count = 2 * BLOCK
    send_pack = jnp.concatenate(
        [send_rows.reshape(group_size, capacity, row_count, features), stat_rows, id_rows], 2
    )
    slot_rows = send_pack.shape[2]
    edges = jnp.concatenate([out_grad[:, 0], out_grad[:, tile_y - 1]], 0)
    send_pack = jnp.concatenate(
        [
            send_pack.reshape(group_size, capacity * slot_rows, features),
            jnp.broadcast_to(edges[None], (group_size,) + edges.shape),
        ],
        1,
    )
    send_pack, diag_rows, diag_stats, diag_keys = lax.optimization_barrier(
        (send_pack, row_pack, stat_blocks, key_pack)
    )
    pack_in = lax.all_to_all(send_pack, "gy", split_axis=0, concat_axis=0, tiled=True)
    diag_query, diag_key, diag_value = tile_grads(diag_rows, diag_stats, diag_keys)
    pack_in, diag_query, diag_key, diag_value = lax.optimization_barrier(
        (pack_in, diag_query, diag_key, diag_value)
    )
    column = lax.axis_index("gy")
    edge_in = pack_in[:, capacity * slot_rows :]
    before_col = lax.dynamic_index_in_dim(edge_in, (column + group_size - 1) % group_size, 0, False)
    after_col = lax.dynamic_index_in_dim(edge_in, (column + 1) % group_size, 0, False)
    before_col = before_col[tile_x:]
    after_col = after_col[:tile_x]
    grad_x, values_x = lax.optimization_barrier((out_grad, values))
    count_x = (lax.axis_size(OUTER) * lax.axis_size(INNER))
    ahead = [(i, (i + 1) % count_x) for i in range(count_x)]
    behind = [((i + 1) % count_x, i) for i in range(count_x)]
    from_before = lax.ppermute(grad_x[tile_x - 1 :], (OUTER, INNER), ahead)
    from_after = lax.ppermute(grad_x[:1], (OUTER, INNER), behind)
    moved = [
        grad_x.astype(jnp.float32),
        jnp.concatenate([grad_x[1:], from_after], 0).astype(jnp.float32),
        jnp.concatenate([from_before, grad_x[:-1]], 0).astype(jnp.float32),
        jnp.concatenate([grad_x[:, 1:], after_col[:, None]], 1).astype(jnp.float32),
        jnp.concatenate([before_col[:, None], grad_x[:, :-1]], 1).astype(jnp.float32),
    ]
    value_float = values_x.astype(jnp.float32)
    stencil_term = stencil[0] * moved[0]
    for index in range(1, 5):
        stencil_term = stencil_term + stencil[index] * moved[index]
    partial_rows = jnp.stack(
        [jnp.sum(moved[index] * value_float, axis=(0, 1)) for index in range(5)]
    )
    point_count = tile_x * tile_y * count_x * group_size
    pack_in = pack_in[:, : capacity * slot_rows].reshape(group_size, capacity, slot_rows, features)
    plane_sum = gather_sum(partial_rows, INNER)
    plane_sum, pack_in = lax.optimization_barrier((plane_sum, pack_in))
    column_sum = gather_sum(plane_sum, OUTER)
    rows_in = pack_in[:, :, :row_count].reshape(group_size, capacity, 2, BLOCK, features)
    stats_in = pack_in[:, :, row_count : row_count + 2 * HEADS].reshape(
        group_size, capacity, 2, HEADS, BLOCK
    )
    ids_in = pack_in[:, :, row_count + 2 * HEADS, 0]
    item_count = rows_in.shape[1]
    total_items = group_size * item_count
    wanted = ids_in.astype(jnp.float32).astype(jnp.int32) - 1
    chooser = (wanted[..., None] == jnp.arange(row_blocks, dtype=jnp.int32)).astype(jnp.bfloat16)
    keys_in = jnp.dot(
        chooser.reshape(-1, row_blocks),
        key_pack.reshape(row_blocks, -1),
        preferred_element_type=jnp.float32,
    )
    keys_in = keys_in.astype(jnp.bfloat16).reshape(total_items, 2, BLOCK, features)
    query_part, key_part, value_part = tile_grads(
        rows_in.reshape(total_items, 2, BLOCK, features),
        stats_in.reshape(total_items, 2, HEADS, BLOCK),
        keys_in,
    )
    query_part = query_part.reshape(group_size, item_count, BLOCK, features)
    key_part = key_part.reshape(group_size, item_count, BLOCK, features)
    value_part = value_part.reshape(group_size, item_count, BLOCK, features)
    stencil_count = partial_rows.shape[0]
    stencil_hi = column_sum.astype(jnp.bfloat16)
    stencil_rest = column_sum - stencil_hi.astype(jnp.float32)
    stencil_mid = stencil_rest.astype(jnp.bfloat16)
    stencil_lo = (stencil_rest - stencil_mid.astype(jnp.float32)).astype(jnp.bfloat16)
    stencil_terms = jnp.concatenate([stencil_hi, stencil_mid, stencil_lo], 0)
    term_rows = 3 * stencil_count
    stencil_pad = jnp.pad(stencil_terms, ((0, 16 - term_rows), (0, 0)))
    return_pack = jnp.concatenate(
        [
            query_part.reshape(group_size, item_count * BLOCK, features).astype(jnp.bfloat16),
            jnp.broadcast_to(stencil_pad[None], (group_size, 16, features)),
        ],
        1,
    )
    return_in = lax.all_to_all(return_pack, "gy", split_axis=0, concat_axis=0, tiled=True)
    returned = return_in[:, : item_count * BLOCK].astype(jnp.float32)
    terms_in = return_in[:, item_count * BLOCK : item_count * BLOCK + term_rows].astype(jnp.float32)
    terms_in = terms_in.reshape(group_size, 3, stencil_count, features)
    summed = jnp.sum(terms_in[:, 0] + terms_in[:, 1] + terms_in[:, 2], 0)
    returned, pieces, ids_in = (returned, jnp.stack([key_part, value_part], 2), ids_in)
    query_sum = diag_query + jnp.einsum(
        "sr,sbf->rbf",
        picker,
        returned.reshape(slot_count, BLOCK, features),
        precision=lax.Precision.HIGHEST,
    )
    arrived = ids_in.reshape(slot_count).astype(jnp.float32).astype(jnp.int32) - 1
    owned = (arrived[:, None] == jnp.arange(row_blocks, dtype=jnp.int32)[None, :]).astype(
        jnp.float32
    )
    key_value_sum = jnp.einsum(
        "sr,sxbf->rxbf",
        owned,
        pieces.reshape(slot_count, 2, BLOCK, features),
        precision=lax.Precision.HIGHEST,
    )
    key_total = diag_key + key_value_sum[:, 0]
    value_total = diag_value + key_value_sum[:, 1]
    stencil_grad = summed / math.sqrt(point_count)
    query_grad = query_sum.reshape(tile_x, tile_y, features).astype(jnp.bfloat16)
    key_grad = key_total.reshape(tile_x, tile_y, features).astype(jnp.bfloat16)
    value_grad = (value_total.reshape(tile_x, tile_y, features) + stencil_term).astype(jnp.bfloat16)
    return (query_grad, key_grad, value_grad, stencil_grad)


def solution(mesh):
    rows = mesh.shape["gx"]
    inner = PLANE if rows % PLANE == 0 else 1
    fine = jax.sharding.Mesh(
        mesh.devices.reshape(rows // inner, inner, mesh.shape["gy"]), (OUTER, INNER, "gy")
    )
    split = (OUTER, INNER)
    placed = (
        P(split, "gy", None),
        P(split, "gy", None),
        P(split, "gy", None),
        P(split, "gy", None),
        P(split, "gy", None),
        P(None, split, "gy"),
        P(split, "gy", None),
        P(),
    )
    return jax.shard_map(
        per_device,
        mesh=fine,
        in_specs=placed,
        out_specs=(P(split, "gy", None), P(split, "gy", None), P(split, "gy", None), P()),
        check_vma=False,
    )
```

```python
import math

import jax
import jax.numpy as jnp
from jax import lax
from jax.sharding import PartitionSpec as P

BLOCK = 128
HEADS = 4
OUTER = "gx_outer"
INNER = "gx_inner"
PLANE = 8


def prime_factors(count):
    factors = []
    base = 2
    while count > 1:
        while count % base == 0:
            factors.append(base)
            count //= base
        base += 1
    return factors


def exchange_sum(value, axis):
    count = lax.axis_size(axis)
    index = lax.axis_index(axis)
    stride = 1
    for radix in prime_factors(count):
        digit = (index // stride) % radix
        if radix == 2:
            pairs = [(i, i + stride) if (i // stride) % 2 == 0 else (i, i - stride) for i in range(count)]
            value = value + lax.ppermute(value, axis, pairs)
        else:
            received = [value]
            for shift in range(1, radix):
                pairs = []
                for i in range(count):
                    d = (i // stride) % radix
                    pairs.append((i, i + (((d + shift) % radix) - d) * stride))
                received.append(lax.ppermute(value, axis, pairs))
            total = None
            for position in range(radix):
                offset = (digit - position) % radix
                term = received[0]
                for shift in range(1, radix):
                    term = jnp.where(offset == shift, received[shift], term)
                total = term if total is None else total + term
            value = total
        stride *= radix
    return value


def gather_sum(value, axis):
    count = lax.axis_size(axis)
    spread = jnp.broadcast_to(value[None], (count,) + value.shape)
    parts = lax.all_to_all(spread, axis, split_axis=0, concat_axis=0, tiled=True)
    return jnp.sum(parts, axis=0)


def tile_grads(row_pack, stat_pack, key_pack):
    features = row_pack.shape[3]
    head_width = features // HEADS
    softmax_scale = 1.0 / math.sqrt(head_width)
    head_of = jnp.arange(features, dtype=jnp.int32) // head_width
    mask = (head_of[None, :] == jnp.arange(HEADS, dtype=jnp.int32)[:, None]).astype(row_pack.dtype)

    def spread(part):
        return part[:, None] * mask[None, :, None, :]

    query_rows = row_pack[:, 0]
    grad_rows = row_pack[:, 1]
    key_rows = key_pack[:, 0]
    value_rows = key_pack[:, 1]
    query_heads = spread(query_rows)
    grad_heads = spread(grad_rows)
    key_heads = spread(key_rows)
    log_part = stat_pack[:, 0].astype(jnp.float32)
    delta_part = stat_pack[:, 1].astype(jnp.float32)
    scores = (
        jnp.einsum("shqf,skf->shqk", query_heads, key_rows, preferred_element_type=jnp.float32)
        * softmax_scale
    )
    weights = jnp.exp(scores - log_part[..., None])
    weight_grad = jnp.einsum(
        "shqf,skf->shqk", grad_heads, value_rows, preferred_element_type=jnp.float32
    )
    score_grad = weights * (weight_grad - delta_part[..., None])
    weights_low = weights.astype(jnp.bfloat16)
    score_low = score_grad.astype(jnp.bfloat16)
    value_part = jnp.einsum(
        "shqk,shqf->skf", weights_low, grad_heads, preferred_element_type=jnp.float32
    )
    key_part = (
        jnp.einsum("shqk,shqf->skf", score_low, query_heads, preferred_element_type=jnp.float32)
        * softmax_scale
    )
    query_part = (
        jnp.einsum("shqk,shkf->sqf", score_low, key_heads, preferred_element_type=jnp.float32)
        * softmax_scale
    )
    return (query_part, key_part, value_part)


def per_device(queries, keys, values, out_attn, out_grad, log_norm, neighbour_blocks, stencil):
    tile_x, tile_y, features = queries.shape
    row_blocks = tile_x * tile_y // BLOCK
    head_width = features // HEADS
    listed = neighbour_blocks.shape[2]
    group_size = lax.axis_size("gy")
    pair_count = row_blocks * listed
    capacity = max(2, (pair_count + group_size - 1) // group_size)
    slot_count = group_size * capacity
    query_blocks = queries.reshape(row_blocks, BLOCK, features)
    key_blocks = keys.reshape(row_blocks, BLOCK, features)
    value_blocks = values.reshape(row_blocks, BLOCK, features)
    grad_blocks = out_grad.reshape(row_blocks, BLOCK, features)
    products = out_grad.astype(jnp.float32) * out_attn.astype(jnp.float32)
    delta = products.reshape(row_blocks, BLOCK, HEADS, head_width).sum(-1).astype(jnp.bfloat16)
    delta = delta.transpose(0, 2, 1)
    norm_blocks = log_norm.reshape(HEADS, row_blocks, BLOCK).transpose(1, 0, 2)
    stat_blocks = jnp.stack([norm_blocks, delta], 1)
    row_pack = jnp.stack([query_blocks, grad_blocks], 1)
    key_pack = jnp.stack([key_blocks, value_blocks], 1)
    point_count = tile_x * tile_y * (lax.axis_size(OUTER) * lax.axis_size(INNER)) * group_size
    columns = neighbour_blocks.reshape(pair_count)
    owners = columns // row_blocks
    inner = columns % row_blocks
    order = jnp.arange(pair_count, dtype=jnp.int32)
    before = (owners[:, None] == owners[None, :]) & (order[None, :] < order[:, None])
    rank = jnp.sum(before.astype(jnp.int32), 1)
    slot_of = owners * capacity + rank
    placed = (jnp.arange(slot_count, dtype=jnp.int32)[:, None] == slot_of[None, :]).astype(
        jnp.float32
    )
    source_rows = (
        (order // listed)[:, None] == jnp.arange(row_blocks, dtype=jnp.int32)[None, :]
    ).astype(jnp.float32)
    picker = jnp.dot(placed, source_rows, precision=lax.Precision.HIGHEST)
    picker_low = picker.astype(jnp.bfloat16)
    send_rows = jnp.dot(
        picker_low, row_pack.reshape(row_blocks, -1), preferred_element_type=jnp.float32
    )
    send_rows = send_rows.astype(jnp.bfloat16).reshape(group_size, capacity, 2, BLOCK, features)
    send_stats = jnp.dot(
        picker_low, stat_blocks.reshape(row_blocks, -1), preferred_element_type=jnp.float32
    )
    send_stats = send_stats.astype(jnp.bfloat16).reshape(group_size, capacity, 2, HEADS, BLOCK)
    send_ids = jnp.dot(placed, (inner + 1).astype(jnp.float32), precision=lax.Precision.HIGHEST)
    send_ids = send_ids.astype(jnp.bfloat16).reshape(group_size, capacity)
    stat_rows = send_stats.reshape(group_size, capacity, 2 * HEADS, BLOCK)
    id_rows = jnp.broadcast_to(send_ids[:, :, None, None], (group_size, capacity, 8, features))
    row_count = 2 * BLOCK
    send_pack = jnp.concatenate(
        [send_rows.reshape(group_size, capacity, row_count, features), stat_rows, id_rows], 2
    )
    slot_rows = send_pack.shape[2]
    target = jnp.arange(group_size, dtype=jnp.int32)[:, None, None]
    upper = (lax.axis_index("gy") + 1) % group_size
    edge_out = jnp.where(target == upper, out_grad[None, :, tile_y - 1], out_grad[None, :, 0])
    send_pack = jnp.concatenate(
        [
            send_pack.reshape(group_size, capacity * slot_rows, features),
            edge_out,
        ],
        1,
    )
    send_pack, diag_rows, diag_stats, diag_keys = lax.optimization_barrier(
        (send_pack, row_pack, stat_blocks, key_pack)
    )
    pack_in = lax.all_to_all(send_pack, "gy", split_axis=0, concat_axis=0, tiled=True)
    diag_query, diag_key, diag_value = tile_grads(diag_rows, diag_stats, diag_keys)
    pack_in, diag_query, diag_key, diag_value = lax.optimization_barrier(
        (pack_in, diag_query, diag_key, diag_value)
    )
    column = lax.axis_index("gy")
    edge_in = pack_in[:, capacity * slot_rows :]
    before_col = lax.dynamic_index_in_dim(edge_in, (column + group_size - 1) % group_size, 0, False)
    after_col = lax.dynamic_index_in_dim(edge_in, (column + 1) % group_size, 0, False)
    grad_x, values_x = lax.optimization_barrier((out_grad, values))
    count_x = (lax.axis_size(OUTER) * lax.axis_size(INNER))
    ahead = [(i, (i + 1) % count_x) for i in range(count_x)]
    behind = [((i + 1) % count_x, i) for i in range(count_x)]
    from_before = lax.ppermute(grad_x[tile_x - 1 :], (OUTER, INNER), ahead)
    from_after = lax.ppermute(grad_x[:1], (OUTER, INNER), behind)
    moved = [
        grad_x.astype(jnp.float32),
        jnp.concatenate([grad_x[1:], from_after], 0).astype(jnp.float32),
        jnp.concatenate([from_before, grad_x[:-1]], 0).astype(jnp.float32),
        jnp.concatenate([grad_x[:, 1:], after_col[:, None]], 1).astype(jnp.float32),
        jnp.concatenate([before_col[:, None], grad_x[:, :-1]], 1).astype(jnp.float32),
    ]
    value_float = values_x.astype(jnp.float32)
    stencil_term = stencil[0] * moved[0]
    for index in range(1, 5):
        stencil_term = stencil_term + stencil[index] * moved[index]
    partial_rows = jnp.stack(
        [jnp.sum(moved[index] * value_float, axis=(0, 1)) for index in range(5)]
    )
    point_count = tile_x * tile_y * count_x * group_size
    pack_in = pack_in[:, : capacity * slot_rows].reshape(group_size, capacity, slot_rows, features)
    plane_sum = gather_sum(partial_rows, INNER)
    plane_sum, pack_in = lax.optimization_barrier((plane_sum, pack_in))
    column_sum = gather_sum(plane_sum, OUTER)
    rows_in = pack_in[:, :, :row_count].reshape(group_size, capacity, 2, BLOCK, features)
    stats_in = pack_in[:, :, row_count : row_count + 2 * HEADS].reshape(
        group_size, capacity, 2, HEADS, BLOCK
    )
    ids_in = pack_in[:, :, row_count + 2 * HEADS, 0]
    item_count = rows_in.shape[1]
    total_items = group_size * item_count
    wanted = ids_in.astype(jnp.float32).astype(jnp.int32) - 1
    chooser = (wanted[..., None] == jnp.arange(row_blocks, dtype=jnp.int32)).astype(jnp.bfloat16)
    keys_in = jnp.dot(
        chooser.reshape(-1, row_blocks),
        key_pack.reshape(row_blocks, -1),
        preferred_element_type=jnp.float32,
    )
    keys_in = keys_in.astype(jnp.bfloat16).reshape(total_items, 2, BLOCK, features)
    query_part, key_part, value_part = tile_grads(
        rows_in.reshape(total_items, 2, BLOCK, features),
        stats_in.reshape(total_items, 2, HEADS, BLOCK),
        keys_in,
    )
    query_part = query_part.reshape(group_size, item_count, BLOCK, features)
    key_part = key_part.reshape(group_size, item_count, BLOCK, features)
    value_part = value_part.reshape(group_size, item_count, BLOCK, features)
    stencil_count = partial_rows.shape[0]
    stencil_hi = column_sum.astype(jnp.bfloat16)
    stencil_rest = column_sum - stencil_hi.astype(jnp.float32)
    stencil_mid = stencil_rest.astype(jnp.bfloat16)
    stencil_lo = (stencil_rest - stencil_mid.astype(jnp.float32)).astype(jnp.bfloat16)
    stencil_terms = jnp.concatenate([stencil_hi, stencil_mid, stencil_lo], 0)
    term_rows = 3 * stencil_count
    stencil_pad = jnp.pad(stencil_terms, ((0, 16 - term_rows), (0, 0)))
    return_pack = jnp.concatenate(
        [
            query_part.reshape(group_size, item_count * BLOCK, features).astype(jnp.bfloat16),
            jnp.broadcast_to(stencil_pad[None], (group_size, 16, features)),
        ],
        1,
    )
    return_in = lax.all_to_all(return_pack, "gy", split_axis=0, concat_axis=0, tiled=True)
    returned = return_in[:, : item_count * BLOCK].astype(jnp.float32)
    terms_in = return_in[:, item_count * BLOCK : item_count * BLOCK + term_rows].astype(jnp.float32)
    terms_in = terms_in.reshape(group_size, 3, stencil_count, features)
    summed = jnp.sum(terms_in[:, 0] + terms_in[:, 1] + terms_in[:, 2], 0)
    returned, pieces, ids_in = (returned, jnp.stack([key_part, value_part], 2), ids_in)
    query_sum = diag_query + jnp.einsum(
        "sr,sbf->rbf",
        picker,
        returned.reshape(slot_count, BLOCK, features),
        precision=lax.Precision.HIGHEST,
    )
    arrived = ids_in.reshape(slot_count).astype(jnp.float32).astype(jnp.int32) - 1
    owned = (arrived[:, None] == jnp.arange(row_blocks, dtype=jnp.int32)[None, :]).astype(
        jnp.float32
    )
    key_value_sum = jnp.einsum(
        "sr,sxbf->rxbf",
        owned,
        pieces.reshape(slot_count, 2, BLOCK, features),
        precision=lax.Precision.HIGHEST,
    )
    key_total = diag_key + key_value_sum[:, 0]
    value_total = diag_value + key_value_sum[:, 1]
    stencil_grad = summed / math.sqrt(point_count)
    query_grad = query_sum.reshape(tile_x, tile_y, features).astype(jnp.bfloat16)
    key_grad = key_total.reshape(tile_x, tile_y, features).astype(jnp.bfloat16)
    value_grad = (value_total.reshape(tile_x, tile_y, features) + stencil_term).astype(jnp.bfloat16)
    return (query_grad, key_grad, value_grad, stencil_grad)


def solution(mesh):
    rows = mesh.shape["gx"]
    inner = PLANE if rows % PLANE == 0 else 1
    fine = jax.sharding.Mesh(
        mesh.devices.reshape(rows // inner, inner, mesh.shape["gy"]), (OUTER, INNER, "gy")
    )
    split = (OUTER, INNER)
    placed = (
        P(split, "gy", None),
        P(split, "gy", None),
        P(split, "gy", None),
        P(split, "gy", None),
        P(split, "gy", None),
        P(None, split, "gy"),
        P(split, "gy", None),
        P(),
    )
    return jax.shard_map(
        per_device,
        mesh=fine,
        in_specs=placed,
        out_specs=(P(split, "gy", None), P(split, "gy", None), P(split, "gy", None), P()),
        check_vma=False,
    )
```
